512 devices in a mesh: win: 8 (over y), lon: 32 (over x, z_lo, core), lat: 2 (over z_hi).
Axes of the slice: x: 4, y: 8, z: 8 (z_hi: 2, z_lo: 4; z = z_hi * 4 + z_lo), core: 2. Of those that a mesh axis runs over, the one named last changes fastest.
Arguments:
- dual_state: float32 [8, 16, 2, 16384], P('win', None, 'lat', 'lon'), may hold values from -6 to 6
- dual_obs: float32 [8, 16, 2, 16384], P('win', None, 'lat', 'lon'), may hold values from -6 to 6
- increment: float32 [8, 16, 2, 16384], P('win', None, 'lat', 'lon'), may hold values from -6 to 6
- resid_dual: float32 [8, 16, 2, 16384], P('win', None, 'lat', 'lon'), may hold values from -6 to 6
- resid_obs: float32 [8, 16, 2, 16384], P('win', None, 'lat', 'lon'), may hold values from -6 to 6
- resid_incr: float32 [8, 16, 2, 16384], P('win', None, 'lat', 'lon'), may hold values from -6 to 6
- search_dual: float32 [8, 16, 2, 16384], P('win', None, 'lat', 'lon'), may hold values from -6 to 6
- search_obs: float32 [8, 16, 2, 16384], P('win', None, 'lat', 'lon'), may hold values from -6 to 6
- search_incr: float32 [8, 16, 2, 16384], P('win', None, 'lat', 'lon'), may hold values from -6 to 6
- ensemble: bfloat16 [8, 64, 16, 2, 16384], P('win', None, None, 'lat', 'lon'), may hold values from -12 to 12
- tangent_coefs: float32 [8, 5, 16, 2, 16384], P('win', None, None, 'lat', 'lon'), may hold values from -0.25 to 0.25
- obs_weight: float32 [8, 16, 2, 16384], P('win', None, 'lat', 'lon'), may hold values from 0.25 to 2
- obs_var: float32 [8, 16, 2, 16384], P('win', None, 'lat', 'lon'), may hold values from 0.5 to 2
- loc_cols: int32 [32, 5], P('lon'), may hold values from 0 to 31, as said below
- loc_vals: bfloat16 [32, 5, 512, 512], P('lon'), may hold values from -0.125 to 0.125
Outputs:
- next_dual: float32 [8, 16, 2, 16384], P('win', None, 'lat', 'lon')
- next_obs: float32 [8, 16, 2, 16384], P('win', None, 'lat', 'lon')
- next_incr: float32 [8, 16, 2, 16384], P('win', None, 'lat', 'lon')
- next_res_dual: float32 [8, 16, 2, 16384], P('win', None, 'lat', 'lon')
- next_res_obs: float32 [8, 16, 2, 16384], P('win', None, 'lat', 'lon')
- next_res_incr: float32 [8, 16, 2, 16384], P('win', None, 'lat', 'lon')
The draws below stay inside these ranges and needn't reach their ends.
Inputs may be any that keep to these rules, and one draw needn't show every extreme that they name: `loc_cols`: row block i names 5 distinct column blocks, block i itself among them, each within 3 blocks of i around the longitude loop.
All inputs are finite; a program needn't handle non-finite values.
Results may differ from the reference program's by a relative error of at most 0.0017.
Values may be sent and summed in bfloat16 or wider, within the bound.
No kernel may reach another device: no remote copies, remote signals or barrier semaphores. Data moves between devices by JAX's collectives and lax.ppermute only.
A program may use at most 64 MiB of HBM per device.

```python
import math
import jax
import jax.numpy as jnp
from jax import lax

LEV = 16
MEM = 64
BLK = 512
NB = 5
REACH = 3
NWIN = 8
NLAT = 2
NBLK = 32
NLON = 16384


def draw_loc_cols(key, part):
    keys = jax.random.split(key, NBLK)

    def one_row(row_key):
        first_key, second_key = jax.random.split(row_key)
        offsets = jnp.concatenate([jnp.arange(-REACH, 0, dtype=jnp.int32), jnp.arange(1, REACH + 1, dtype=jnp.int32)])
        picked = jax.random.permutation(first_key, offsets)[:NB - 1]
        chosen = jnp.concatenate([jnp.zeros((1,), jnp.int32), picked])
        return jax.random.permutation(second_key, chosen).astype(jnp.int32)
    offsets = jax.vmap(one_row)(keys)
    rows = jnp.arange(NBLK, dtype=jnp.int32)[:, None]
    return ((rows + offsets + NBLK) % NBLK).astype(jnp.int32)


def level_of(stream_key, dims, cuts, smallest, largest):
    def one(axis_at, blocks):
        draws = jax.random.uniform(jax.random.fold_in(jax.random.fold_in(stream_key, 6), axis_at), (blocks,), jnp.float32, smallest / len(cuts), largest / len(cuts))
        return jnp.repeat(jnp.exp(draws), dims[axis_at] // blocks).reshape((-1,) + (1,) * (len(dims) - axis_at - 1))

    gain = one(*cuts[0])
    for cut in cuts[1:]:
        gain = gain * one(*cut)
    return gain


def centred(rng, dims, width, limit, pieces=(), held_as=jnp.bfloat16):
    gain = level_of(rng, dims, pieces, -0.22, 0.18) if pieces else 1.0
    result = jax.random.normal(rng, dims, jnp.float32) * width * gain
    return jnp.minimum(jnp.maximum(result, -limit), limit).astype(held_as)


def setup_inputs(seed: int = 0) -> dict:
    key_of = jax.random.split(jax.random.key(seed), 16)
    return {
        "dual_state": centred(key_of[0], (NWIN, LEV, NLAT, NLON), 1.0, 6.0, ((0, 8), (2, 2), (3, 32)), jnp.float32),
        "dual_obs": centred(key_of[1], (NWIN, LEV, NLAT, NLON), 1.0, 6.0, ((0, 8), (2, 2), (3, 32)), jnp.float32),
        "increment": centred(key_of[2], (NWIN, LEV, NLAT, NLON), 1.0, 6.0, ((0, 8), (2, 2), (3, 32)), jnp.float32),
        "resid_dual": centred(key_of[3], (NWIN, LEV, NLAT, NLON), 1.0, 6.0, ((0, 8), (2, 2), (3, 32)), jnp.float32),
        "resid_obs": centred(key_of[4], (NWIN, LEV, NLAT, NLON), 1.0, 6.0, ((0, 8), (2, 2), (3, 32)), jnp.float32),
        "resid_incr": centred(key_of[5], (NWIN, LEV, NLAT, NLON), 1.0, 6.0, ((0, 8), (2, 2), (3, 32)), jnp.float32),
        "search_dual": centred(key_of[6], (NWIN, LEV, NLAT, NLON), 1.0, 6.0, ((0, 8), (2, 2), (3, 32)), jnp.float32),
        "search_obs": centred(key_of[7], (NWIN, LEV, NLAT, NLON), 1.0, 6.0, ((0, 8), (2, 2), (3, 32)), jnp.float32),
        "search_incr": centred(key_of[8], (NWIN, LEV, NLAT, NLON), 1.0, 6.0, ((0, 8), (2, 2), (3, 32)), jnp.float32),
        "ensemble": centred(key_of[9], (NWIN, MEM, LEV, NLAT, NLON), 2.0, 12.0, ((0, 8), (3, 2), (4, 32))),
        "tangent_coefs": jnp.clip(jax.random.uniform(key_of[10], (NWIN, 5, LEV, NLAT, NLON), jnp.float32, -0.25, 0.25) * level_of(key_of[10], (NWIN, 5, LEV, NLAT, NLON), ((0, 8), (3, 2), (4, 32)), -0.4, 0.0), -0.25, 0.25),
        "obs_weight": jnp.clip(jnp.exp(math.log(2.0) - 2.0794415 * jax.random.uniform(key_of[11], (NWIN, LEV, NLAT, NLON), jnp.float32) ** level_of(key_of[11], (NWIN, LEV, NLAT, NLON), ((0, 8), (2, 2), (3, 32)), -0.2, 0.2)), 0.25, 2.0),
        "obs_var": jnp.clip(jnp.exp(math.log(2.0) - 1.3862944 * jax.random.uniform(key_of[12], (NWIN, LEV, NLAT, NLON), jnp.float32) ** level_of(key_of[12], (NWIN, LEV, NLAT, NLON), ((0, 8), (2, 2), (3, 32)), -0.2, 0.2)), 0.5, 2.0),
        "loc_cols": draw_loc_cols(jax.random.fold_in(key_of[15], 71), 0),
        "loc_vals": centred(key_of[14], (NBLK, NB, BLK, BLK), (BLK * NB) ** -0.5, 0.125, ((0, 32),)),
    }


def east(field):
    return jnp.roll(field, -1, axis=-1)


def west(field):
    return jnp.roll(field, 1, axis=-1)


def north(field):
    return jnp.concatenate([field[..., 1:, :], jnp.zeros_like(field[..., :1, :])], axis=-2)


def south(field):
    return jnp.concatenate([jnp.zeros_like(field[..., :1, :]), field[..., :-1, :]], axis=-2)


def tangent(field, coefs):
    return ((0.5 + coefs[:, 0]) * field + coefs[:, 1] * east(field) + coefs[:, 2] * west(field)
            + coefs[:, 3] * north(field) + coefs[:, 4] * south(field))


def adjoint(field, coefs):
    return ((0.5 + coefs[:, 0]) * field + west(coefs[:, 1] * field) + east(coefs[:, 2] * field)
            + south(coefs[:, 3] * field) + north(coefs[:, 4] * field))


def reference(dual_state, dual_obs, increment, resid_dual, resid_obs, resid_incr,
              search_dual, search_obs, search_incr, ensemble, tangent_coefs,
              obs_weight, obs_var, loc_cols, loc_vals):
    moved = tangent(tangent(search_incr, tangent_coefs), tangent_coefs)
    backed = adjoint(adjoint(search_dual, tangent_coefs), tangent_coefs)
    prior = jnp.concatenate([jnp.zeros_like(moved[:1]), moved[:-1]], axis=0)
    later = jnp.concatenate([backed[1:], jnp.zeros_like(backed[:1])], axis=0)
    tiles = loc_vals.astype(jnp.float32)

    def localize(pair):
        members, search = pair
        products = (members.astype(jnp.float32) * search[None]).astype(jnp.bfloat16)
        blocks = products.reshape(MEM * LEV * NLAT, NBLK, BLK).astype(jnp.float32)
        spread = jnp.zeros(blocks.shape, jnp.float32)
        for column in range(NB):
            source = jnp.take(blocks, loc_cols[:, column], axis=1)
            spread = spread + jnp.einsum("rbq,bqp->rbp", source, tiles[:, column])
        spread = spread.reshape(MEM, LEV, NLAT, NLON)
        return jnp.sum(members.astype(jnp.float32) * spread, axis=0) / (MEM - 1)

    covar = lax.map(localize, (ensemble, search_dual))
    image_dual = covar + search_incr - prior
    image_obs = obs_var * search_obs + obs_weight * search_incr
    image_incr = search_dual - later + obs_weight * search_obs
    resid_sq = jnp.sum(resid_dual * resid_dual) + jnp.sum(resid_obs * resid_obs) + jnp.sum(resid_incr * resid_incr)
    search_sq = jnp.sum(search_dual * search_dual) + jnp.sum(search_obs * search_obs) + jnp.sum(search_incr * search_incr)
    alpha = resid_sq / (search_sq + 1e-6)
    return (dual_state + alpha * search_dual, dual_obs + alpha * search_obs, increment + alpha * search_incr,
            resid_dual - alpha * image_dual, resid_obs - alpha * image_obs, resid_incr - alpha * image_incr)
```

```python
import jax
import jax.numpy as jnp
from jax import lax
from jax.sharding import PartitionSpec as P

REACH = 3


def from_offset(value, axis, distance):
    count = lax.axis_size(axis)
    return lax.ppermute(value, axis, [((i + distance) % count, i) for i in range(count)])


def shifted(value, axis, steps):
    count = lax.axis_size(axis)
    leading, last = (max(0, -steps), min(count, count - steps))
    return lax.ppermute(value, axis, [(source, source + steps) for source in range(leading, last)])


def lon_extended(packed, width):
    left = from_offset(packed[..., -width:], "lon", -1)
    right = from_offset(packed[..., :width], "lon", 1)
    return jnp.concatenate([left, packed, right], axis=-1)


def lat_partner(value):
    return lax.ppermute(value, "lat", [(0, 1), (1, 0)])


def forward_pair(f_a, f_b, c_a, cn_a):
    return (
        (0.5 + c_a[0, :, 1:-1]) * f_a[:, 1:-1]
        + c_a[1, :, 1:-1] * f_a[:, 2:]
        + c_a[2, :, 1:-1] * f_a[:, :-2]
        + cn_a[:, 1:-1] * f_b[:, 1:-1]
    )


def adjoint_pair(f_a, f_b, c_a, ca_a):
    return (
        (0.5 + c_a[0, :, 1:-1]) * f_a[:, 1:-1]
        + (c_a[1] * f_a)[:, :-2]
        + (c_a[2] * f_a)[:, 2:]
        + ca_a[:, 1:-1] * f_b[:, 1:-1]
    )


def propagate_both(own, other, first_row):
    u_a, w_a, c_a = own[0], own[1], own[2:]
    u_b, w_b, c_b = other[0], other[1], other[2:]
    cn_a = jnp.where(first_row, c_a[3], c_a[4])
    cn_b = jnp.where(first_row, c_b[4], c_b[3])
    ca_a = jnp.where(first_row, c_b[4], c_b[3])
    ca_b = jnp.where(first_row, c_a[3], c_a[4])
    s_a = forward_pair(u_a, u_b, c_a, cn_a)
    s_b = forward_pair(u_b, u_a, c_b, cn_b)
    moved = forward_pair(s_a, s_b, c_a[:, :, 1:-1], cn_a[:, 1:-1])
    t_a = adjoint_pair(w_a, w_b, c_a, ca_a)
    t_b = adjoint_pair(w_b, w_a, c_b, ca_b)
    backed = adjoint_pair(t_a, t_b, c_a[:, :, 1:-1], ca_a[:, 1:-1])
    return moved, backed


def localize(members, search, loc_cols, loc_vals):
    count_members = members.shape[0]
    block = members.shape[-1]
    products = (members.astype(jnp.float32) * search[None]).astype(jnp.bfloat16)
    flat = products.reshape(-1, block)
    bands = lax.axis_size("lon")
    here = lax.axis_index("lon")
    columns = loc_cols[0]
    tiles = loc_vals[0]
    offsets = [0]
    for distance in range(1, REACH + 1):
        offsets += [distance, -distance]
    sources = {0: flat}
    for offset in offsets[1:]:
        sources[offset] = from_offset(flat, "lon", offset)

    def weight_for(offset):
        target = (here + offset + bands) % bands
        match = columns == target
        picked = tiles[jnp.argmax(match)]
        return jnp.where(jnp.any(match), picked, jnp.zeros_like(picked))

    total = jnp.dot(flat, weight_for(0), preferred_element_type=jnp.float32)
    for offset in offsets[1:]:
        total = total + jnp.dot(sources[offset], weight_for(offset), preferred_element_type=jnp.float32)
    spread = total.reshape(products.shape)
    return jnp.sum(members.astype(jnp.float32) * spread, axis=0) / (count_members - 1)


def local(
    dual_state,
    dual_obs,
    increment,
    resid_dual,
    resid_obs,
    resid_incr,
    search_dual,
    search_obs,
    search_incr,
    ensemble,
    tangent_coefs,
    obs_weight,
    obs_var,
    loc_cols,
    loc_vals,
):
    resid_local = (
        jnp.sum(resid_dual * resid_dual)
        + jnp.sum(resid_obs * resid_obs)
        + jnp.sum(resid_incr * resid_incr)
    )
    search_local = (
        jnp.sum(search_dual * search_dual)
        + jnp.sum(search_obs * search_obs)
        + jnp.sum(search_incr * search_incr)
    )
    sums = lax.psum(lax.psum(lax.psum(jnp.stack([resid_local, search_local]), "lat"), "lon"), "win")
    alpha = sums[0] / (sums[1] + 1e-06)

    packed = jnp.concatenate(
        [search_incr[0, :, 0][None], search_dual[0, :, 0][None], tangent_coefs[0, :, :, 0]], axis=0
    )
    own = lon_extended(packed, 2)
    other = lat_partner(own)
    first_row = lax.axis_index("lat") == 0
    moved, backed = propagate_both(own, other, first_row)
    earlier = shifted(moved, "win", 1)[None, :, None]
    following = shifted(backed, "win", -1)[None, :, None]

    covar = localize(ensemble[0, :, :, 0], search_dual[0, :, 0], loc_cols, loc_vals)[None, :, None]
    image_dual = covar + search_incr - earlier
    image_obs = obs_var * search_obs + obs_weight * search_incr
    image_incr = search_dual - following + obs_weight * search_obs
    return (
        dual_state + alpha * search_dual,
        dual_obs + alpha * search_obs,
        increment + alpha * search_incr,
        resid_dual - alpha * image_dual,
        resid_obs - alpha * image_obs,
        resid_incr - alpha * image_incr,
    )


def solution(mesh):
    field = P("win", None, "lat", "lon")
    stacked = P("win", None, None, "lat", "lon")
    placed = (
        field, field, field, field, field, field, field, field, field,
        stacked, stacked, field, field,
        P("lon", None),
        P("lon", None, None, None),
    )
    return jax.shard_map(
        local,
        mesh=mesh,
        in_specs=placed,
        out_specs=(field,) * 6,
        check_vma=False,
    )
```

```python
import jax
import jax.numpy as jnp
from jax import lax
from jax.sharding import PartitionSpec as P

REACH = 3


def from_offset(value, axis, distance):
    count = lax.axis_size(axis)
    return lax.ppermute(value, axis, [((i + distance) % count, i) for i in range(count)])


def shifted(value, axis, steps):
    count = lax.axis_size(axis)
    leading, last = (max(0, -steps), min(count, count - steps))
    return lax.ppermute(value, axis, [(source, source + steps) for source in range(leading, last)])


def lon_extended(packed, width):
    left = from_offset(packed[..., -width:], "lon", -1)
    right = from_offset(packed[..., :width], "lon", 1)
    return jnp.concatenate([left, packed, right], axis=-1)


def lat_partner(value):
    return lax.ppermute(value, "lat", [(0, 1), (1, 0)])


def forward_pair(f_a, f_b, c_a, cn_a):
    return (
        (0.5 + c_a[0, :, 1:-1]) * f_a[:, 1:-1]
        + c_a[1, :, 1:-1] * f_a[:, 2:]
        + c_a[2, :, 1:-1] * f_a[:, :-2]
        + cn_a[:, 1:-1] * f_b[:, 1:-1]
    )


def adjoint_pair(f_a, f_b, c_a, ca_a):
    return (
        (0.5 + c_a[0, :, 1:-1]) * f_a[:, 1:-1]
        + (c_a[1] * f_a)[:, :-2]
        + (c_a[2] * f_a)[:, 2:]
        + ca_a[:, 1:-1] * f_b[:, 1:-1]
    )


def propagate_both(own, other, first_row):
    u_a, w_a, c_a = own[0], own[1], own[2:]
    u_b, w_b, c_b = other[0], other[1], other[2:]
    cn_a = jnp.where(first_row, c_a[3], c_a[4])
    cn_b = jnp.where(first_row, c_b[4], c_b[3])
    ca_a = jnp.where(first_row, c_b[4], c_b[3])
    ca_b = jnp.where(first_row, c_a[3], c_a[4])
    s_a = forward_pair(u_a, u_b, c_a, cn_a)
    s_b = forward_pair(u_b, u_a, c_b, cn_b)
    moved = forward_pair(s_a, s_b, c_a[:, :, 1:-1], cn_a[:, 1:-1])
    t_a = adjoint_pair(w_a, w_b, c_a, ca_a)
    t_b = adjoint_pair(w_b, w_a, c_b, ca_b)
    backed = adjoint_pair(t_a, t_b, c_a[:, :, 1:-1], ca_a[:, 1:-1])
    return moved, backed


def localize(members, search, loc_cols, loc_vals):
    count_members = members.shape[0]
    block = members.shape[-1]
    products = (members.astype(jnp.float32) * search[None]).astype(jnp.bfloat16)
    flat = products.reshape(-1, block)
    bands = lax.axis_size("lon")
    here = lax.axis_index("lon")
    columns = loc_cols[0]
    tiles = loc_vals[0]
    offsets = [0]
    for distance in range(1, REACH + 1):
        offsets += [distance, -distance]
    sources = {0: flat}
    for offset in offsets[1:]:
        sources[offset] = from_offset(flat, "lon", offset)

    def weight_for(offset):
        target = (here + offset + bands) % bands
        match = columns == target
        picked = tiles[jnp.argmax(match)]
        return jnp.where(jnp.any(match), picked, jnp.zeros_like(picked))

    total = jnp.dot(flat, weight_for(0), preferred_element_type=jnp.float32)
    for offset in offsets[1:]:
        total = total + jnp.dot(sources[offset], weight_for(offset), preferred_element_type=jnp.float32)
    spread = total.reshape(products.shape)
    return jnp.sum(members.astype(jnp.float32) * spread, axis=0) / (count_members - 1)


def local(
    dual_state,
    dual_obs,
    increment,
    resid_dual,
    resid_obs,
    resid_incr,
    search_dual,
    search_obs,
    search_incr,
    ensemble,
    tangent_coefs,
    obs_weight,
    obs_var,
    loc_cols,
    loc_vals,
):
    resid_local = (
        jnp.sum(resid_dual * resid_dual)
        + jnp.sum(resid_obs * resid_obs)
        + jnp.sum(resid_incr * resid_incr)
    )
    search_local = (
        jnp.sum(search_dual * search_dual)
        + jnp.sum(search_obs * search_obs)
        + jnp.sum(search_incr * search_incr)
    )
    wide = jnp.broadcast_to(jnp.stack([resid_local, search_local])[:, None], (2, 8192))
    sums = lax.psum(wide, ("win", "lon", "lat"))[:, 0]
    alpha = sums[0] / (sums[1] + 1e-06)

    packed = jnp.concatenate(
        [search_incr[0, :, 0][None], search_dual[0, :, 0][None], tangent_coefs[0, :, :, 0]], axis=0
    )
    own = lon_extended(packed, 2)
    other = lat_partner(own)
    first_row = lax.axis_index("lat") == 0
    moved, backed = propagate_both(own, other, first_row)
    earlier = shifted(moved, "win", 1)[None, :, None]
    following = shifted(backed, "win", -1)[None, :, None]

    covar = localize(ensemble[0, :, :, 0], search_dual[0, :, 0], loc_cols, loc_vals)[None, :, None]
    image_dual = covar + search_incr - earlier
    image_obs = obs_var * search_obs + obs_weight * search_incr
    image_incr = search_dual - following + obs_weight * search_obs
    return (
        dual_state + alpha * search_dual,
        dual_obs + alpha * search_obs,
        increment + alpha * search_incr,
        resid_dual - alpha * image_dual,
        resid_obs - alpha * image_obs,
        resid_incr - alpha * image_incr,
    )


def solution(mesh):
    field = P("win", None, "lat", "lon")
    stacked = P("win", None, None, "lat", "lon")
    placed = (
        field, field, field, field, field, field, field, field, field,
        stacked, stacked, field, field,
        P("lon", None),
        P("lon", None, None, None),
    )
    return jax.shard_map(
        local,
        mesh=mesh,
        in_specs=placed,
        out_specs=(field,) * 6,
        check_vma=False,
    )
```

```python
import jax
import jax.numpy as jnp
from jax import lax
from jax.sharding import PartitionSpec as P

REACH = 3


def from_offset(value, axis, distance):
    count = lax.axis_size(axis)
    return lax.ppermute(value, axis, [((i + distance) % count, i) for i in range(count)])


def shifted(value, axis, steps):
    count = lax.axis_size(axis)
    leading, last = (max(0, -steps), min(count, count - steps))
    return lax.ppermute(value, axis, [(source, source + steps) for source in range(leading, last)])


def butterfly_sum(value, axes):
    for axis in axes:
        count = lax.axis_size(axis)
        step = 1
        while step < count:
            value = value + lax.ppermute(value, axis, [(i, i ^ step) for i in range(count)])
            step *= 2
    return value


def lon_extended(packed, width):
    left = from_offset(packed[..., -width:], "lon", -1)
    right = from_offset(packed[..., :width], "lon", 1)
    return jnp.concatenate([left, packed, right], axis=-1)


def lat_partner(value):
    return lax.ppermute(value, "lat", [(0, 1), (1, 0)])


def forward_pair(f_a, f_b, c_a, cn_a):
    return (
        (0.5 + c_a[0, :, 1:-1]) * f_a[:, 1:-1]
        + c_a[1, :, 1:-1] * f_a[:, 2:]
        + c_a[2, :, 1:-1] * f_a[:, :-2]
        + cn_a[:, 1:-1] * f_b[:, 1:-1]
    )


def adjoint_pair(f_a, f_b, c_a, ca_a):
    return (
        (0.5 + c_a[0, :, 1:-1]) * f_a[:, 1:-1]
        + (c_a[1] * f_a)[:, :-2]
        + (c_a[2] * f_a)[:, 2:]
        + ca_a[:, 1:-1] * f_b[:, 1:-1]
    )


def propagate_both(own, other, first_row):
    u_a, w_a, c_a = own[0], own[1], own[2:]
    u_b, w_b, c_b = other[0], other[1], other[2:]
    cn_a = jnp.where(first_row, c_a[3], c_a[4])
    cn_b = jnp.where(first_row, c_b[4], c_b[3])
    ca_a = jnp.where(first_row, c_b[4], c_b[3])
    ca_b = jnp.where(first_row, c_a[3], c_a[4])
    s_a = forward_pair(u_a, u_b, c_a, cn_a)
    s_b = forward_pair(u_b, u_a, c_b, cn_b)
    moved = forward_pair(s_a, s_b, c_a[:, :, 1:-1], cn_a[:, 1:-1])
    t_a = adjoint_pair(w_a, w_b, c_a, ca_a)
    t_b = adjoint_pair(w_b, w_a, c_b, ca_b)
    backed = adjoint_pair(t_a, t_b, c_a[:, :, 1:-1], ca_a[:, 1:-1])
    return moved, backed


def localize(members, search, loc_cols, loc_vals):
    count_members = members.shape[0]
    block = members.shape[-1]
    products = (members.astype(jnp.float32) * search[None]).astype(jnp.bfloat16)
    flat = products.reshape(-1, block)
    bands = lax.axis_size("lon")
    here = lax.axis_index("lon")
    columns = loc_cols[0]
    tiles = loc_vals[0]
    offsets = [0]
    for distance in range(1, REACH + 1):
        offsets += [distance, -distance]
    sources = {0: flat}
    for offset in offsets[1:]:
        sources[offset] = from_offset(flat, "lon", offset)

    def weight_for(offset):
        target = (here + offset + bands) % bands
        match = columns == target
        picked = tiles[jnp.argmax(match)]
        return jnp.where(jnp.any(match), picked, jnp.zeros_like(picked))

    total = jnp.dot(flat, weight_for(0), preferred_element_type=jnp.float32)
    for offset in offsets[1:]:
        total = total + jnp.dot(sources[offset], weight_for(offset), preferred_element_type=jnp.float32)
    spread = total.reshape(products.shape)
    return jnp.sum(members.astype(jnp.float32) * spread, axis=0) / (count_members - 1)


def local(
    dual_state,
    dual_obs,
    increment,
    resid_dual,
    resid_obs,
    resid_incr,
    search_dual,
    search_obs,
    search_incr,
    ensemble,
    tangent_coefs,
    obs_weight,
    obs_var,
    loc_cols,
    loc_vals,
):
    resid_local = (
        jnp.sum(resid_dual * resid_dual)
        + jnp.sum(resid_obs * resid_obs)
        + jnp.sum(resid_incr * resid_incr)
    )
    search_local = (
        jnp.sum(search_dual * search_dual)
        + jnp.sum(search_obs * search_obs)
        + jnp.sum(search_incr * search_incr)
    )
    sums = butterfly_sum(jnp.stack([resid_local, search_local]), ("lon", "lat", "win"))
    alpha = sums[0] / (sums[1] + 1e-06)

    packed = jnp.concatenate(
        [search_incr[0, :, 0][None], search_dual[0, :, 0][None], tangent_coefs[0, :, :, 0]], axis=0
    )
    own = lon_extended(packed, 2)
    other = lat_partner(own)
    first_row = lax.axis_index("lat") == 0
    moved, backed = propagate_both(own, other, first_row)
    earlier = shifted(moved, "win", 1)[None, :, None]
    following = shifted(backed, "win", -1)[None, :, None]

    covar = localize(ensemble[0, :, :, 0], search_dual[0, :, 0], loc_cols, loc_vals)[None, :, None]
    image_dual = covar + search_incr - earlier
    image_obs = obs_var * search_obs + obs_weight * search_incr
    image_incr = search_dual - following + obs_weight * search_obs
    return (
        dual_state + alpha * search_dual,
        dual_obs + alpha * search_obs,
        increment + alpha * search_incr,
        resid_dual - alpha * image_dual,
        resid_obs - alpha * image_obs,
        resid_incr - alpha * image_incr,
    )


def solution(mesh):
    field = P("win", None, "lat", "lon")
    stacked = P("win", None, None, "lat", "lon")
    placed = (
        field, field, field, field, field, field, field, field, field,
        stacked, stacked, field, field,
        P("lon", None),
        P("lon", None, None, None),
    )
    return jax.shard_map(
        local,
        mesh=mesh,
        in_specs=placed,
        out_specs=(field,) * 6,
        check_vma=False,
    )
```

```python
import jax
import jax.numpy as jnp
from jax import lax
from jax.sharding import PartitionSpec as P

REACH = 3


def from_offset(value, axis, distance):
    count = lax.axis_size(axis)
    return lax.ppermute(value, axis, [((i + distance) % count, i) for i in range(count)])


def shifted(value, axis, steps):
    count = lax.axis_size(axis)
    leading, last = (max(0, -steps), min(count, count - steps))
    return lax.ppermute(value, axis, [(source, source + steps) for source in range(leading, last)])


def butterfly_sum(value, axes):
    for axis in axes:
        count = lax.axis_size(axis)
        step = 1
        while step < count:
            value = value + lax.ppermute(value, axis, [(i, i ^ step) for i in range(count)])
            step *= 2
    return value


def lon_extended(packed, width):
    left = from_offset(packed[..., -width:], "lon", -1)
    right = from_offset(packed[..., :width], "lon", 1)
    return jnp.concatenate([left, packed, right], axis=-1)


def lat_partner(value):
    return lax.ppermute(value, "lat", [(0, 1), (1, 0)])


def forward_pair(f_a, f_b, c_a, cn_a):
    return (
        (0.5 + c_a[0, :, 1:-1]) * f_a[:, 1:-1]
        + c_a[1, :, 1:-1] * f_a[:, 2:]
        + c_a[2, :, 1:-1] * f_a[:, :-2]
        + cn_a[:, 1:-1] * f_b[:, 1:-1]
    )


def adjoint_pair(f_a, f_b, c_a, ca_a):
    return (
        (0.5 + c_a[0, :, 1:-1]) * f_a[:, 1:-1]
        + (c_a[1] * f_a)[:, :-2]
        + (c_a[2] * f_a)[:, 2:]
        + ca_a[:, 1:-1] * f_b[:, 1:-1]
    )


def propagate_both(own, other, first_row):
    u_a, w_a, c_a = own[0], own[1], own[2:]
    u_b, w_b, c_b = other[0], other[1], other[2:]
    cn_a = jnp.where(first_row, c_a[3], c_a[4])
    cn_b = jnp.where(first_row, c_b[4], c_b[3])
    ca_a = jnp.where(first_row, c_b[4], c_b[3])
    ca_b = jnp.where(first_row, c_a[3], c_a[4])
    s_a = forward_pair(u_a, u_b, c_a, cn_a)
    s_b = forward_pair(u_b, u_a, c_b, cn_b)
    moved = forward_pair(s_a, s_b, c_a[:, :, 1:-1], cn_a[:, 1:-1])
    t_a = adjoint_pair(w_a, w_b, c_a, ca_a)
    t_b = adjoint_pair(w_b, w_a, c_b, ca_b)
    backed = adjoint_pair(t_a, t_b, c_a[:, :, 1:-1], ca_a[:, 1:-1])
    return moved, backed


def localize(members, search, loc_cols, loc_vals, partials):
    count_members = members.shape[0]
    block = members.shape[-1]
    products = (members.astype(jnp.float32) * search[None]).astype(jnp.bfloat16)
    flat = products.reshape(-1, block)
    bands = lax.axis_size("lon")
    here = lax.axis_index("lon")
    columns = loc_cols[0]
    tiles = loc_vals[0]
    offsets = [0]
    for distance in range(1, REACH + 1):
        offsets += [distance, -distance]
    sources = {0: flat}
    for offset in offsets[1:]:
        sources[offset] = from_offset(flat, "lon", offset)

    def weight_for(offset):
        target = (here + offset + bands) % bands
        match = columns == target
        picked = tiles[jnp.argmax(match)]
        return jnp.where(jnp.any(match), picked, jnp.zeros_like(picked))

    partials, _ = lax.optimization_barrier((partials, [sources[offset] for offset in offsets[1:]]))
    total = jnp.dot(flat, weight_for(0), preferred_element_type=jnp.float32)
    for offset in offsets[1:]:
        total = total + jnp.dot(sources[offset], weight_for(offset), preferred_element_type=jnp.float32)
    spread = total.reshape(products.shape)
    return jnp.sum(members.astype(jnp.float32) * spread, axis=0) / (count_members - 1), partials


def local(
    dual_state,
    dual_obs,
    increment,
    resid_dual,
    resid_obs,
    resid_incr,
    search_dual,
    search_obs,
    search_incr,
    ensemble,
    tangent_coefs,
    obs_weight,
    obs_var,
    loc_cols,
    loc_vals,
):
    resid_local = (
        jnp.sum(resid_dual * resid_dual)
        + jnp.sum(resid_obs * resid_obs)
        + jnp.sum(resid_incr * resid_incr)
    )
    search_local = (
        jnp.sum(search_dual * search_dual)
        + jnp.sum(search_obs * search_obs)
        + jnp.sum(search_incr * search_incr)
    )

    packed = jnp.concatenate(
        [search_incr[0, :, 0][None], search_dual[0, :, 0][None], tangent_coefs[0, :, :, 0]], axis=0
    )
    own = lon_extended(packed, 2)
    other = lat_partner(own)
    first_row = lax.axis_index("lat") == 0
    moved, backed = propagate_both(own, other, first_row)
    earlier = shifted(moved, "win", 1)[None, :, None]
    following = shifted(backed, "win", -1)[None, :, None]

    covar, partials = localize(
        ensemble[0, :, :, 0], search_dual[0, :, 0], loc_cols, loc_vals, jnp.stack([resid_local, search_local])
    )
    covar = covar[None, :, None]
    partials, _ = lax.optimization_barrier((partials, other))
    sums = butterfly_sum(partials, ("lon", "lat", "win"))
    alpha = sums[0] / (sums[1] + 1e-06)
    image_dual = covar + search_incr - earlier
    image_obs = obs_var * search_obs + obs_weight * search_incr
    image_incr = search_dual - following + obs_weight * search_obs
    return (
        dual_state + alpha * search_dual,
        dual_obs + alpha * search_obs,
        increment + alpha * search_incr,
        resid_dual - alpha * image_dual,
        resid_obs - alpha * image_obs,
        resid_incr - alpha * image_incr,
    )


def solution(mesh):
    field = P("win", None, "lat", "lon")
    stacked = P("win", None, None, "lat", "lon")
    placed = (
        field, field, field, field, field, field, field, field, field,
        stacked, stacked, field, field,
        P("lon", None),
        P("lon", None, None, None),
    )
    return jax.shard_map(
        local,
        mesh=mesh,
        in_specs=placed,
        out_specs=(field,) * 6,
        check_vma=False,
    )
```

```python
import jax
import jax.numpy as jnp
from jax import lax
from jax.sharding import PartitionSpec as P

REACH = 3


def from_offset(value, axis, distance):
    count = lax.axis_size(axis)
    return lax.ppermute(value, axis, [((i + distance) % count, i) for i in range(count)])


def shifted(value, axis, steps):
    count = lax.axis_size(axis)
    leading, last = (max(0, -steps), min(count, count - steps))
    return lax.ppermute(value, axis, [(source, source + steps) for source in range(leading, last)])


def butterfly_sum(value, axes):
    for axis in axes:
        count = lax.axis_size(axis)
        step = 1
        while step < count:
            value = value + lax.ppermute(value, axis, [(i, i ^ step) for i in range(count)])
            step *= 2
    return value


def lon_extended(packed, width):
    left = from_offset(packed[..., -width:], "lon", -1)
    right = from_offset(packed[..., :width], "lon", 1)
    return jnp.concatenate([left, packed, right], axis=-1)


def lat_partner(value):
    return lax.ppermute(value, "lat", [(0, 1), (1, 0)])


def forward_pair(f_a, f_b, c_a, cn_a):
    return (
        (0.5 + c_a[0, :, 1:-1]) * f_a[:, 1:-1]
        + c_a[1, :, 1:-1] * f_a[:, 2:]
        + c_a[2, :, 1:-1] * f_a[:, :-2]
        + cn_a[:, 1:-1] * f_b[:, 1:-1]
    )


def adjoint_pair(f_a, f_b, c_a, ca_a):
    return (
        (0.5 + c_a[0, :, 1:-1]) * f_a[:, 1:-1]
        + (c_a[1] * f_a)[:, :-2]
        + (c_a[2] * f_a)[:, 2:]
        + ca_a[:, 1:-1] * f_b[:, 1:-1]
    )


def propagate_both(own, other, first_row):
    u_a, w_a, c_a = own[0], own[1], own[2:]
    u_b, w_b, c_b = other[0], other[1], other[2:]
    cn_a = jnp.where(first_row, c_a[3], c_a[4])
    cn_b = jnp.where(first_row, c_b[4], c_b[3])
    ca_a = jnp.where(first_row, c_b[4], c_b[3])
    ca_b = jnp.where(first_row, c_a[3], c_a[4])
    s_a = forward_pair(u_a, u_b, c_a, cn_a)
    s_b = forward_pair(u_b, u_a, c_b, cn_b)
    moved = forward_pair(s_a, s_b, c_a[:, :, 1:-1], cn_a[:, 1:-1])
    t_a = adjoint_pair(w_a, w_b, c_a, ca_a)
    t_b = adjoint_pair(w_b, w_a, c_b, ca_b)
    backed = adjoint_pair(t_a, t_b, c_a[:, :, 1:-1], ca_a[:, 1:-1])
    return moved, backed


def localize(members, search, loc_cols, loc_vals, partials):
    count_members = members.shape[0]
    block = members.shape[-1]
    products = (members.astype(jnp.float32) * search[None]).astype(jnp.bfloat16)
    flat = products.reshape(-1, block)
    rows = flat.shape[0]
    bands = lax.axis_size("lon")
    here = lax.axis_index("lon")
    even = here % 2 == 0
    columns = loc_cols[0]
    tiles = loc_vals[0]
    partner = [(i, i ^ 1) for i in range(bands)]
    beside = lax.ppermute(flat, "lon", partner)
    ahead = from_offset(flat, "lon", 2)
    behind = from_offset(flat, "lon", -2)
    far = lax.ppermute(flat, "lon", [(s, (s + 3) % bands if s % 2 else (s - 3) % bands) for s in range(bands)])
    relayed = lax.ppermute(jnp.concatenate([ahead, behind], axis=0), "lon", partner)
    received = [
        (beside, jnp.where(even, 1, -1)),
        (ahead, 2),
        (behind, -2),
        (far, jnp.where(even, -3, 3)),
        (relayed[:rows], jnp.where(even, 3, 1)),
        (relayed[rows:], jnp.where(even, -1, -3)),
    ]

    def weight_for(offset):
        target = (here + offset + bands) % bands
        match = columns == target
        picked = tiles[jnp.argmax(match)]
        return jnp.where(jnp.any(match), picked, jnp.zeros_like(picked))

    partials, _ = lax.optimization_barrier((partials, [value for value, _ in received]))
    total = jnp.dot(flat, weight_for(0), preferred_element_type=jnp.float32)
    for value, offset in received:
        total = total + jnp.dot(value, weight_for(offset), preferred_element_type=jnp.float32)
    spread = total.reshape(products.shape)
    return jnp.sum(members.astype(jnp.float32) * spread, axis=0) / (count_members - 1), partials


def local(
    dual_state,
    dual_obs,
    increment,
    resid_dual,
    resid_obs,
    resid_incr,
    search_dual,
    search_obs,
    search_incr,
    ensemble,
    tangent_coefs,
    obs_weight,
    obs_var,
    loc_cols,
    loc_vals,
):
    resid_local = (
        jnp.sum(resid_dual * resid_dual)
        + jnp.sum(resid_obs * resid_obs)
        + jnp.sum(resid_incr * resid_incr)
    )
    search_local = (
        jnp.sum(search_dual * search_dual)
        + jnp.sum(search_obs * search_obs)
        + jnp.sum(search_incr * search_incr)
    )

    packed = jnp.concatenate(
        [search_incr[0, :, 0][None], search_dual[0, :, 0][None], tangent_coefs[0, :, :, 0]], axis=0
    )
    own = lon_extended(packed, 2)
    other = lat_partner(own)
    first_row = lax.axis_index("lat") == 0
    moved, backed = propagate_both(own, other, first_row)
    earlier = shifted(moved, "win", 1)[None, :, None]
    following = shifted(backed, "win", -1)[None, :, None]

    covar, partials = localize(
        ensemble[0, :, :, 0],
        search_dual[0, :, 0],
        loc_cols,
        loc_vals,
        butterfly_sum(jnp.stack([resid_local, search_local]), ("win",)),
    )
    covar = covar[None, :, None]
    partials, _ = lax.optimization_barrier((partials, other))
    sums = butterfly_sum(partials, ("lon", "lat"))
    alpha = sums[0] / (sums[1] + 1e-06)
    image_dual = covar + search_incr - earlier
    image_obs = obs_var * search_obs + obs_weight * search_incr
    image_incr = search_dual - following + obs_weight * search_obs
    return (
        dual_state + alpha * search_dual,
        dual_obs + alpha * search_obs,
        increment + alpha * search_incr,
        resid_dual - alpha * image_dual,
        resid_obs - alpha * image_obs,
        resid_incr - alpha * image_incr,
    )


def solution(mesh):
    field = P("win", None, "lat", "lon")
    stacked = P("win", None, None, "lat", "lon")
    placed = (
        field, field, field, field, field, field, field, field, field,
        stacked, stacked, field, field,
        P("lon", None),
        P("lon", None, None, None),
    )
    return jax.shard_map(
        local,
        mesh=mesh,
        in_specs=placed,
        out_specs=(field,) * 6,
        check_vma=False,
    )
```

```python
import jax
import jax.numpy as jnp
from jax import lax
from jax.sharding import PartitionSpec as P

REACH = 3


def from_offset(value, axis, distance):
    count = lax.axis_size(axis)
    return lax.ppermute(value, axis, [((i + distance) % count, i) for i in range(count)])


def shifted(value, axis, steps):
    count = lax.axis_size(axis)
    leading, last = (max(0, -steps), min(count, count - steps))
    return lax.ppermute(value, axis, [(source, source + steps) for source in range(leading, last)])


def butterfly_sum(value, axes, first=1):
    for axis in axes:
        count = lax.axis_size(axis)
        step = first
        while step < count:
            value = value + lax.ppermute(value, axis, [(i, i ^ step) for i in range(count)])
            step *= 2
    return value


def lon_extended(packed, width, extra):
    left = from_offset(jnp.concatenate([packed[..., -width:], extra]), "lon", -1)
    right = from_offset(jnp.concatenate([packed[..., :width], extra]), "lon", 1)
    return jnp.concatenate([left[:-1], packed, right[:-1]], axis=-1), left[-1], right[-1]


def lat_partner(value):
    return lax.ppermute(value, "lat", [(0, 1), (1, 0)])


def forward_pair(f_a, f_b, c_a, cn_a):
    return (
        (0.5 + c_a[0, :, 1:-1]) * f_a[:, 1:-1]
        + c_a[1, :, 1:-1] * f_a[:, 2:]
        + c_a[2, :, 1:-1] * f_a[:, :-2]
        + cn_a[:, 1:-1] * f_b[:, 1:-1]
    )


def adjoint_pair(f_a, f_b, c_a, ca_a):
    return (
        (0.5 + c_a[0, :, 1:-1]) * f_a[:, 1:-1]
        + (c_a[1] * f_a)[:, :-2]
        + (c_a[2] * f_a)[:, 2:]
        + ca_a[:, 1:-1] * f_b[:, 1:-1]
    )


def propagate_both(own, other, first_row):
    u_a, w_a, c_a = own[0], own[1], own[2:]
    u_b, w_b, c_b = other[0], other[1], other[2:]
    cn_a = jnp.where(first_row, c_a[3], c_a[4])
    cn_b = jnp.where(first_row, c_b[4], c_b[3])
    ca_a = jnp.where(first_row, c_b[4], c_b[3])
    ca_b = jnp.where(first_row, c_a[3], c_a[4])
    s_a = forward_pair(u_a, u_b, c_a, cn_a)
    s_b = forward_pair(u_b, u_a, c_b, cn_b)
    moved = forward_pair(s_a, s_b, c_a[:, :, 1:-1], cn_a[:, 1:-1])
    t_a = adjoint_pair(w_a, w_b, c_a, ca_a)
    t_b = adjoint_pair(w_b, w_a, c_b, ca_b)
    backed = adjoint_pair(t_a, t_b, c_a[:, :, 1:-1], ca_a[:, 1:-1])
    return moved, backed


def localize(members, search, loc_cols, loc_vals, partials):
    count_members = members.shape[0]
    block = members.shape[-1]
    products = (members.astype(jnp.float32) * search[None]).astype(jnp.bfloat16)
    flat = products.reshape(-1, block)
    rows = flat.shape[0]
    bands = lax.axis_size("lon")
    here = lax.axis_index("lon")
    even = here % 2 == 0
    columns = loc_cols[0]
    tiles = loc_vals[0]
    partner = [(i, i ^ 1) for i in range(bands)]
    beside = lax.ppermute(flat, "lon", partner)
    ahead = from_offset(flat, "lon", 2)
    behind = from_offset(flat, "lon", -2)
    far = lax.ppermute(flat, "lon", [(s, (s + 3) % bands if s % 2 else (s - 3) % bands) for s in range(bands)])
    relayed = lax.ppermute(jnp.concatenate([ahead, behind], axis=0), "lon", partner)
    received = [
        (beside, jnp.where(even, 1, -1)),
        (ahead, 2),
        (behind, -2),
        (far, jnp.where(even, -3, 3)),
        (relayed[:rows], jnp.where(even, 3, 1)),
        (relayed[rows:], jnp.where(even, -1, -3)),
    ]

    def weight_for(offset):
        target = (here + offset + bands) % bands
        match = columns == target
        picked = tiles[jnp.argmax(match)]
        return jnp.where(jnp.any(match), picked, jnp.zeros_like(picked))

    partials, _ = lax.optimization_barrier((partials, [value for value, _ in received]))
    total = jnp.dot(flat, weight_for(0), preferred_element_type=jnp.float32)
    for value, offset in received:
        total = total + jnp.dot(value, weight_for(offset), preferred_element_type=jnp.float32)
    spread = total.reshape(products.shape)
    return jnp.sum(members.astype(jnp.float32) * spread, axis=0) / (count_members - 1), partials


def local(
    dual_state,
    dual_obs,
    increment,
    resid_dual,
    resid_obs,
    resid_incr,
    search_dual,
    search_obs,
    search_incr,
    ensemble,
    tangent_coefs,
    obs_weight,
    obs_var,
    loc_cols,
    loc_vals,
):
    resid_local = (
        jnp.sum(resid_dual * resid_dual)
        + jnp.sum(resid_obs * resid_obs)
        + jnp.sum(resid_incr * resid_incr)
    )
    search_local = (
        jnp.sum(search_dual * search_dual)
        + jnp.sum(search_obs * search_obs)
        + jnp.sum(search_incr * search_incr)
    )

    packed = jnp.concatenate(
        [search_incr[0, :, 0][None], search_dual[0, :, 0][None], tangent_coefs[0, :, :, 0]], axis=0
    )
    partial = jnp.stack([resid_local, search_local])
    rider = jnp.broadcast_to(partial[None, None, :], (1,) + packed.shape[1:2] + (2,))
    own, from_left, from_right = lon_extended(packed, 2, rider)
    even = lax.axis_index("lon") % 2 == 0
    partial = partial + jnp.where(even, from_right[0], from_left[0])
    partial = butterfly_sum(partial, ("win",))
    rider = jnp.broadcast_to(jnp.pad(partial, (0, own.shape[-1] - 2))[None, None, :], (1,) + own.shape[1:])
    other = lat_partner(jnp.concatenate([own, rider]))
    partial = partial + other[-1, 0, :2]
    other = other[:-1]
    first_row = lax.axis_index("lat") == 0
    moved, backed = propagate_both(own, other, first_row)
    earlier = shifted(moved, "win", 1)[None, :, None]
    following = shifted(backed, "win", -1)[None, :, None]

    covar, partials = localize(
        ensemble[0, :, :, 0],
        search_dual[0, :, 0],
        loc_cols,
        loc_vals,
        partial,
    )
    covar = covar[None, :, None]
    sums = butterfly_sum(partials, ("lon",), first=2)
    alpha = sums[0] / (sums[1] + 1e-06)
    image_dual = covar + search_incr - earlier
    image_obs = obs_var * search_obs + obs_weight * search_incr
    image_incr = search_dual - following + obs_weight * search_obs
    return (
        dual_state + alpha * search_dual,
        dual_obs + alpha * search_obs,
        increment + alpha * search_incr,
        resid_dual - alpha * image_dual,
        resid_obs - alpha * image_obs,
        resid_incr - alpha * image_incr,
    )


def solution(mesh):
    field = P("win", None, "lat", "lon")
    stacked = P("win", None, None, "lat", "lon")
    placed = (
        field, field, field, field, field, field, field, field, field,
        stacked, stacked, field, field,
        P("lon", None),
        P("lon", None, None, None),
    )
    return jax.shard_map(
        local,
        mesh=mesh,
        in_specs=placed,
        out_specs=(field,) * 6,
        check_vma=False,
    )
```

```python
import jax
import jax.numpy as jnp
from jax import lax
from jax.sharding import PartitionSpec as P

REACH = 3


def from_offset(value, axis, distance):
    count = lax.axis_size(axis)
    return lax.ppermute(value, axis, [((i + distance) % count, i) for i in range(count)])


def shifted(value, axis, steps):
    count = lax.axis_size(axis)
    leading, last = (max(0, -steps), min(count, count - steps))
    return lax.ppermute(value, axis, [(source, source + steps) for source in range(leading, last)])


def butterfly_sum(value, axes, first=1):
    for axis in axes:
        count = lax.axis_size(axis)
        step = first
        while step < count:
            value = value + lax.ppermute(value, axis, [(i, i ^ step) for i in range(count)])
            step *= 2
    return value


def lon_extended(packed, width, extra):
    left = from_offset(jnp.concatenate([packed[..., -width:], extra]), "lon", -1)
    right = from_offset(jnp.concatenate([packed[..., :width], extra]), "lon", 1)
    return jnp.concatenate([left[:-1], packed, right[:-1]], axis=-1), left[-1], right[-1]


def lat_partner(value):
    return lax.ppermute(value, "lat", [(0, 1), (1, 0)])


def forward_pair(f_a, f_b, c_a, cn_a):
    return (
        (0.5 + c_a[0, :, 1:-1]) * f_a[:, 1:-1]
        + c_a[1, :, 1:-1] * f_a[:, 2:]
        + c_a[2, :, 1:-1] * f_a[:, :-2]
        + cn_a[:, 1:-1] * f_b[:, 1:-1]
    )


def adjoint_pair(f_a, f_b, c_a, ca_a):
    return (
        (0.5 + c_a[0, :, 1:-1]) * f_a[:, 1:-1]
        + (c_a[1] * f_a)[:, :-2]
        + (c_a[2] * f_a)[:, 2:]
        + ca_a[:, 1:-1] * f_b[:, 1:-1]
    )


def propagate_both(own, other, first_row):
    u_a, w_a, c_a = own[0], own[1], own[2:]
    u_b, w_b, c_b = other[0], other[1], other[2:]
    cn_a = jnp.where(first_row, c_a[3], c_a[4])
    cn_b = jnp.where(first_row, c_b[4], c_b[3])
    ca_a = jnp.where(first_row, c_b[4], c_b[3])
    ca_b = jnp.where(first_row, c_a[3], c_a[4])
    s_a = forward_pair(u_a, u_b, c_a, cn_a)
    s_b = forward_pair(u_b, u_a, c_b, cn_b)
    moved = forward_pair(s_a, s_b, c_a[:, :, 1:-1], cn_a[:, 1:-1])
    t_a = adjoint_pair(w_a, w_b, c_a, ca_a)
    t_b = adjoint_pair(w_b, w_a, c_b, ca_b)
    backed = adjoint_pair(t_a, t_b, c_a[:, :, 1:-1], ca_a[:, 1:-1])
    return moved, backed


def localize(members, search, loc_cols, loc_vals, partials):
    count_members = members.shape[0]
    block = members.shape[-1]
    products = (members.astype(jnp.float32) * search[None]).astype(jnp.bfloat16)
    flat = products.reshape(-1, block)
    rows = flat.shape[0]
    bands = lax.axis_size("lon")
    here = lax.axis_index("lon")
    even = here % 2 == 0
    columns = loc_cols[0]
    tiles = loc_vals[0]
    partner = [(i, i ^ 1) for i in range(bands)]
    ahead = from_offset(flat, "lon", 2)
    behind = from_offset(flat, "lon", -2)
    far = lax.ppermute(flat, "lon", [(s, (s + 3) % bands if s % 2 else (s - 3) % bands) for s in range(bands)])
    relayed = lax.ppermute(jnp.concatenate([flat, ahead, behind], axis=0), "lon", partner)
    received = [
        (ahead, 2),
        (behind, -2),
        (far, jnp.where(even, -3, 3)),
        (relayed[:rows], jnp.where(even, 1, -1)),
        (relayed[rows : 2 * rows], jnp.where(even, 3, 1)),
        (relayed[2 * rows :], jnp.where(even, -1, -3)),
    ]

    def weight_for(offset):
        target = (here + offset + bands) % bands
        match = columns == target
        picked = tiles[jnp.argmax(match)]
        return jnp.where(jnp.any(match), picked, jnp.zeros_like(picked))

    partials, _ = lax.optimization_barrier((partials, [value for value, _ in received]))
    total = jnp.dot(flat, weight_for(0), preferred_element_type=jnp.float32)
    for value, offset in received:
        total = total + jnp.dot(value, weight_for(offset), preferred_element_type=jnp.float32)
    spread = total.reshape(products.shape)
    return jnp.sum(members.astype(jnp.float32) * spread, axis=0) / (count_members - 1), partials


def local(
    dual_state,
    dual_obs,
    increment,
    resid_dual,
    resid_obs,
    resid_incr,
    search_dual,
    search_obs,
    search_incr,
    ensemble,
    tangent_coefs,
    obs_weight,
    obs_var,
    loc_cols,
    loc_vals,
):
    resid_local = (
        jnp.sum(resid_dual * resid_dual)
        + jnp.sum(resid_obs * resid_obs)
        + jnp.sum(resid_incr * resid_incr)
    )
    search_local = (
        jnp.sum(search_dual * search_dual)
        + jnp.sum(search_obs * search_obs)
        + jnp.sum(search_incr * search_incr)
    )

    packed = jnp.concatenate(
        [search_incr[0, :, 0][None], search_dual[0, :, 0][None], tangent_coefs[0, :, :, 0]], axis=0
    )
    partial = jnp.stack([resid_local, search_local])
    rider = jnp.broadcast_to(partial[None, None, :], (1,) + packed.shape[1:2] + (2,))
    own, from_left, from_right = lon_extended(packed, 2, rider)
    even = lax.axis_index("lon") % 2 == 0
    partial = partial + jnp.where(even, from_right[0], from_left[0])
    partial = butterfly_sum(partial, ("win",))
    rider = jnp.broadcast_to(jnp.pad(partial, (0, own.shape[-1] - 2))[None, None, :], (1,) + own.shape[1:])
    other = lat_partner(jnp.concatenate([own, rider]))
    partial = partial + other[-1, 0, :2]
    other = other[:-1]
    first_row = lax.axis_index("lat") == 0
    moved, backed = propagate_both(own, other, first_row)
    earlier = shifted(moved, "win", 1)[None, :, None]
    following = shifted(backed, "win", -1)[None, :, None]

    covar, partials = localize(
        ensemble[0, :, :, 0],
        search_dual[0, :, 0],
        loc_cols,
        loc_vals,
        partial,
    )
    covar = covar[None, :, None]
    sums = butterfly_sum(partials, ("lon",), first=2)
    alpha = sums[0] / (sums[1] + 1e-06)
    image_dual = covar + search_incr - earlier
    image_obs = obs_var * search_obs + obs_weight * search_incr
    image_incr = search_dual - following + obs_weight * search_obs
    return (
        dual_state + alpha * search_dual,
        dual_obs + alpha * search_obs,
        increment + alpha * search_incr,
        resid_dual - alpha * image_dual,
        resid_obs - alpha * image_obs,
        resid_incr - alpha * image_incr,
    )


def solution(mesh):
    field = P("win", None, "lat", "lon")
    stacked = P("win", None, None, "lat", "lon")
    placed = (
        field, field, field, field, field, field, field, field, field,
        stacked, stacked, field, field,
        P("lon", None),
        P("lon", None, None, None),
    )
    return jax.shard_map(
        local,
        mesh=mesh,
        in_specs=placed,
        out_specs=(field,) * 6,
        check_vma=False,
    )
```

```python
import jax
import jax.numpy as jnp
from jax import lax
from jax.sharding import PartitionSpec as P

REACH = 3


def from_offset(value, axis, distance):
    count = lax.axis_size(axis)
    return lax.ppermute(value, axis, [((i + distance) % count, i) for i in range(count)])


def shifted(value, axis, steps):
    count = lax.axis_size(axis)
    leading, last = (max(0, -steps), min(count, count - steps))
    return lax.ppermute(value, axis, [(source, source + steps) for source in range(leading, last)])


def butterfly_sum(value, axes):
    for axis in axes:
        count = lax.axis_size(axis)
        step = 1
        while step < count:
            value = value + lax.ppermute(value, axis, [(i, i ^ step) for i in range(count)])
            step *= 2
    return value


def lon_extended(packed, width):
    left = from_offset(packed[..., -width:], "lon", -1)
    right = from_offset(packed[..., :width], "lon", 1)
    return jnp.concatenate([left, packed, right], axis=-1)


def lat_partner(value):
    return lax.ppermute(value, "lat", [(0, 1), (1, 0)])


def propagate_both(own, first_row):
    u_a, w_a, c_a = own[0], own[1], own[2:]
    k_a = jnp.where(first_row, c_a[3], c_a[4])
    sent = lat_partner(jnp.stack([u_a[:, 1:-1], (k_a * w_a)[:, 1:-1]]))
    u_b, g_b = sent[0], sent[1]
    s_a = (
        (0.5 + c_a[0, :, 1:-1]) * u_a[:, 1:-1]
        + c_a[1, :, 1:-1] * u_a[:, 2:]
        + c_a[2, :, 1:-1] * u_a[:, :-2]
        + k_a[:, 1:-1] * u_b
    )
    t_a = (
        (0.5 + c_a[0, :, 1:-1]) * w_a[:, 1:-1]
        + (c_a[1] * w_a)[:, :-2]
        + (c_a[2] * w_a)[:, 2:]
        + g_b
    )
    sent = lat_partner(jnp.stack([s_a[:, 1:-1], (k_a[:, 1:-1] * t_a)[:, 1:-1]]))
    s_b, h_b = sent[0], sent[1]
    moved = (
        (0.5 + c_a[0, :, 2:-2]) * s_a[:, 1:-1]
        + c_a[1, :, 2:-2] * s_a[:, 2:]
        + c_a[2, :, 2:-2] * s_a[:, :-2]
        + k_a[:, 2:-2] * s_b
    )
    backed = (
        (0.5 + c_a[0, :, 2:-2]) * t_a[:, 1:-1]
        + (c_a[1, :, 1:-1] * t_a)[:, :-2]
        + (c_a[2, :, 1:-1] * t_a)[:, 2:]
        + h_b
    )
    return moved, backed


def localize(members, search, loc_cols, loc_vals, partials):
    count_members = members.shape[0]
    block = members.shape[-1]
    products = (members.astype(jnp.float32) * search[None]).astype(jnp.bfloat16)
    flat = products.reshape(-1, block)
    rows = flat.shape[0]
    bands = lax.axis_size("lon")
    here = lax.axis_index("lon")
    even = here % 2 == 0
    columns = loc_cols[0]
    tiles = loc_vals[0]
    partner = [(i, i ^ 1) for i in range(bands)]
    beside = lax.ppermute(flat, "lon", partner)
    ahead = from_offset(flat, "lon", 2)
    behind = from_offset(flat, "lon", -2)
    far = lax.ppermute(flat, "lon", [(s, (s + 3) % bands if s % 2 else (s - 3) % bands) for s in range(bands)])
    relayed = lax.ppermute(jnp.concatenate([ahead, behind], axis=0), "lon", partner)
    received = [
        (beside, jnp.where(even, 1, -1)),
        (ahead, 2),
        (behind, -2),
        (far, jnp.where(even, -3, 3)),
        (relayed[:rows], jnp.where(even, 3, 1)),
        (relayed[rows:], jnp.where(even, -1, -3)),
    ]

    def weight_for(offset):
        target = (here + offset + bands) % bands
        match = columns == target
        picked = tiles[jnp.argmax(match)]
        return jnp.where(jnp.any(match), picked, jnp.zeros_like(picked))

    partials, _ = lax.optimization_barrier((partials, [value for value, _ in received]))
    total = jnp.dot(flat, weight_for(0), preferred_element_type=jnp.float32)
    for value, offset in received:
        total = total + jnp.dot(value, weight_for(offset), preferred_element_type=jnp.float32)
    spread = total.reshape(products.shape)
    return jnp.sum(members.astype(jnp.float32) * spread, axis=0) / (count_members - 1), partials


def local(
    dual_state,
    dual_obs,
    increment,
    resid_dual,
    resid_obs,
    resid_incr,
    search_dual,
    search_obs,
    search_incr,
    ensemble,
    tangent_coefs,
    obs_weight,
    obs_var,
    loc_cols,
    loc_vals,
):
    resid_local = (
        jnp.sum(resid_dual * resid_dual)
        + jnp.sum(resid_obs * resid_obs)
        + jnp.sum(resid_incr * resid_incr)
    )
    search_local = (
        jnp.sum(search_dual * search_dual)
        + jnp.sum(search_obs * search_obs)
        + jnp.sum(search_incr * search_incr)
    )

    packed = jnp.concatenate(
        [search_incr[0, :, 0][None], search_dual[0, :, 0][None], tangent_coefs[0, :, :, 0]], axis=0
    )
    own = lon_extended(packed, 2)
    first_row = lax.axis_index("lat") == 0
    moved, backed = propagate_both(own, first_row)
    earlier = shifted(moved, "win", 1)[None, :, None]
    following = shifted(backed, "win", -1)[None, :, None]

    covar, partials = localize(
        ensemble[0, :, :, 0],
        search_dual[0, :, 0],
        loc_cols,
        loc_vals,
        butterfly_sum(jnp.stack([resid_local, search_local]), ("win",)),
    )
    covar = covar[None, :, None]
    partials, _, _ = lax.optimization_barrier((partials, moved, backed))
    sums = butterfly_sum(partials, ("lon", "lat"))
    alpha = sums[0] / (sums[1] + 1e-06)
    image_dual = covar + search_incr - earlier
    image_obs = obs_var * search_obs + obs_weight * search_incr
    image_incr = search_dual - following + obs_weight * search_obs
    return (
        dual_state + alpha * search_dual,
        dual_obs + alpha * search_obs,
        increment + alpha * search_incr,
        resid_dual - alpha * image_dual,
        resid_obs - alpha * image_obs,
        resid_incr - alpha * image_incr,
    )


def solution(mesh):
    field = P("win", None, "lat", "lon")
    stacked = P("win", None, None, "lat", "lon")
    placed = (
        field, field, field, field, field, field, field, field, field,
        stacked, stacked, field, field,
        P("lon", None),
        P("lon", None, None, None),
    )
    return jax.shard_map(
        local,
        mesh=mesh,
        in_specs=placed,
        out_specs=(field,) * 6,
        check_vma=False,
    )
```

```python
import jax
import jax.numpy as jnp
from jax import lax
from jax.sharding import PartitionSpec as P

REACH = 3


def from_offset(value, axis, distance):
    count = lax.axis_size(axis)
    return lax.ppermute(value, axis, [((i + distance) % count, i) for i in range(count)])


def shifted(value, axis, steps):
    count = lax.axis_size(axis)
    leading, last = (max(0, -steps), min(count, count - steps))
    return lax.ppermute(value, axis, [(source, source + steps) for source in range(leading, last)])


def butterfly_sum(value, axes):
    for axis in axes:
        count = lax.axis_size(axis)
        step = 1
        while step < count:
            value = value + lax.ppermute(value, axis, [(i, i ^ step) for i in range(count)])
            step *= 2
    return value


def lon_extended(packed, width):
    left = from_offset(packed[..., -width:], "lon", -1)
    right = from_offset(packed[..., :width], "lon", 1)
    return jnp.concatenate([left, packed, right], axis=-1)


def lat_partner(value):
    return lax.ppermute(value, "lat", [(0, 1), (1, 0)])


def forward_pair(f_a, f_b, c_a, cn_a):
    return (
        (0.5 + c_a[0, :, 1:-1]) * f_a[:, 1:-1]
        + c_a[1, :, 1:-1] * f_a[:, 2:]
        + c_a[2, :, 1:-1] * f_a[:, :-2]
        + cn_a[:, 1:-1] * f_b[:, 1:-1]
    )


def adjoint_pair(f_a, f_b, c_a, ca_a):
    return (
        (0.5 + c_a[0, :, 1:-1]) * f_a[:, 1:-1]
        + (c_a[1] * f_a)[:, :-2]
        + (c_a[2] * f_a)[:, 2:]
        + ca_a[:, 1:-1] * f_b[:, 1:-1]
    )


def propagate_both(own, other, first_row):
    u_a, w_a, c_a = own[0], own[1], own[2:]
    u_b, w_b, c_b = other[0], other[1], other[2:]
    cn_a = jnp.where(first_row, c_a[3], c_a[4])
    cn_b = jnp.where(first_row, c_b[4], c_b[3])
    ca_a = jnp.where(first_row, c_b[4], c_b[3])
    ca_b = jnp.where(first_row, c_a[3], c_a[4])
    s_a = forward_pair(u_a, u_b, c_a, cn_a)
    s_b = forward_pair(u_b, u_a, c_b, cn_b)
    moved = forward_pair(s_a, s_b, c_a[:, :, 1:-1], cn_a[:, 1:-1])
    t_a = adjoint_pair(w_a, w_b, c_a, ca_a)
    t_b = adjoint_pair(w_b, w_a, c_b, ca_b)
    backed = adjoint_pair(t_a, t_b, c_a[:, :, 1:-1], ca_a[:, 1:-1])
    return moved, backed


def localize(members, search, loc_cols, loc_vals, partials):
    count_members = members.shape[0]
    block = members.shape[-1]
    products = (members.astype(jnp.float32) * search[None]).astype(jnp.bfloat16)
    flat = products.reshape(-1, block)
    rows = flat.shape[0]
    bands = lax.axis_size("lon")
    here = lax.axis_index("lon")
    even = here % 2 == 0
    columns = loc_cols[0]
    tiles = loc_vals[0]
    partner = [(i, i ^ 1) for i in range(bands)]
    beside = lax.ppermute(flat, "lon", partner)
    ahead = from_offset(flat, "lon", 2)
    behind = from_offset(flat, "lon", -2)
    far = lax.ppermute(flat, "lon", [(s, (s + 3) % bands if s % 2 else (s - 3) % bands) for s in range(bands)])
    relayed_ahead = lax.ppermute(ahead, "lon", partner)
    relayed_behind = lax.ppermute(behind, "lon", partner)
    received = [
        (beside, jnp.where(even, 1, -1)),
        (ahead, 2),
        (behind, -2),
        (far, jnp.where(even, -3, 3)),
        (relayed_ahead, jnp.where(even, 3, 1)),
        (relayed_behind, jnp.where(even, -1, -3)),
    ]

    def weight_for(offset):
        target = (here + offset + bands) % bands
        match = columns == target
        picked = tiles[jnp.argmax(match)]
        return jnp.where(jnp.any(match), picked, jnp.zeros_like(picked))

    partials, _ = lax.optimization_barrier((partials, [value for value, _ in received[:4]]))
    total = jnp.dot(flat, weight_for(0), preferred_element_type=jnp.float32)
    for value, offset in received:
        total = total + jnp.dot(value, weight_for(offset), preferred_element_type=jnp.float32)
    spread = total.reshape(products.shape)
    return jnp.sum(members.astype(jnp.float32) * spread, axis=0) / (count_members - 1), partials


def local(
    dual_state,
    dual_obs,
    increment,
    resid_dual,
    resid_obs,
    resid_incr,
    search_dual,
    search_obs,
    search_incr,
    ensemble,
    tangent_coefs,
    obs_weight,
    obs_var,
    loc_cols,
    loc_vals,
):
    resid_local = (
        jnp.sum(resid_dual * resid_dual)
        + jnp.sum(resid_obs * resid_obs)
        + jnp.sum(resid_incr * resid_incr)
    )
    search_local = (
        jnp.sum(search_dual * search_dual)
        + jnp.sum(search_obs * search_obs)
        + jnp.sum(search_incr * search_incr)
    )

    packed = jnp.concatenate(
        [search_incr[0, :, 0][None], search_dual[0, :, 0][None], tangent_coefs[0, :, :, 0]], axis=0
    )
    own = lon_extended(packed, 2)
    other = lat_partner(own)
    first_row = lax.axis_index("lat") == 0
    moved, backed = propagate_both(own, other, first_row)
    earlier = shifted(moved, "win", 1)[None, :, None]
    following = shifted(backed, "win", -1)[None, :, None]

    covar, partials = localize(
        ensemble[0, :, :, 0],
        search_dual[0, :, 0],
        loc_cols,
        loc_vals,
        butterfly_sum(jnp.stack([resid_local, search_local]), ("win",)),
    )
    covar = covar[None, :, None]
    partials, _ = lax.optimization_barrier((partials, other))
    sums = butterfly_sum(partials, ("lon", "lat"))
    alpha = sums[0] / (sums[1] + 1e-06)
    image_dual = covar + search_incr - earlier
    image_obs = obs_var * search_obs + obs_weight * search_incr
    image_incr = search_dual - following + obs_weight * search_obs
    return (
        dual_state + alpha * search_dual,
        dual_obs + alpha * search_obs,
        increment + alpha * search_incr,
        resid_dual - alpha * image_dual,
        resid_obs - alpha * image_obs,
        resid_incr - alpha * image_incr,
    )


def solution(mesh):
    field = P("win", None, "lat", "lon")
    stacked = P("win", None, None, "lat", "lon")
    placed = (
        field, field, field, field, field, field, field, field, field,
        stacked, stacked, field, field,
        P("lon", None),
        P("lon", None, None, None),
    )
    return jax.shard_map(
        local,
        mesh=mesh,
        in_specs=placed,
        out_specs=(field,) * 6,
        check_vma=False,
    )
```

```python
import jax
import jax.numpy as jnp
from jax import lax
from jax.sharding import PartitionSpec as P

REACH = 3


def from_offset(value, axis, distance):
    count = lax.axis_size(axis)
    return lax.ppermute(value, axis, [((i + distance) % count, i) for i in range(count)])


def shifted(value, axis, steps):
    count = lax.axis_size(axis)
    leading, last = (max(0, -steps), min(count, count - steps))
    return lax.ppermute(value, axis, [(source, source + steps) for source in range(leading, last)])


def butterfly_sum(value, axes):
    for axis in axes:
        count = lax.axis_size(axis)
        step = 1
        while step < count:
            value = value + lax.ppermute(value, axis, [(i, i ^ step) for i in range(count)])
            step *= 2
    return value


def lon_extended(packed, width):
    left = from_offset(packed[..., -width:], "lon", -1)
    right = from_offset(packed[..., :width], "lon", 1)
    return jnp.concatenate([left, packed, right], axis=-1)


def lat_partner(value):
    return lax.ppermute(value, "lat", [(0, 1), (1, 0)])


def forward_pair(f_a, f_b, c_a, cn_a):
    return (
        (0.5 + c_a[0, :, 1:-1]) * f_a[:, 1:-1]
        + c_a[1, :, 1:-1] * f_a[:, 2:]
        + c_a[2, :, 1:-1] * f_a[:, :-2]
        + cn_a[:, 1:-1] * f_b[:, 1:-1]
    )


def adjoint_pair(f_a, f_b, c_a, ca_a):
    return (
        (0.5 + c_a[0, :, 1:-1]) * f_a[:, 1:-1]
        + (c_a[1] * f_a)[:, :-2]
        + (c_a[2] * f_a)[:, 2:]
        + ca_a[:, 1:-1] * f_b[:, 1:-1]
    )


def propagate_both(own, other, first_row):
    u_a, w_a, c_a = own[0], own[1], own[2:]
    u_b, w_b, c_b, k_b = other[0], other[1], other[2:5], other[5]
    cn_a = coupling(own[2:], first_row)
    cn_b = k_b
    ca_a = k_b
    ca_b = cn_a
    s_a = forward_pair(u_a, u_b, c_a, cn_a)
    s_b = forward_pair(u_b, u_a, c_b, cn_b)
    moved = forward_pair(s_a, s_b, c_a[:, :, 1:-1], cn_a[:, 1:-1])
    t_a = adjoint_pair(w_a, w_b, c_a, ca_a)
    t_b = adjoint_pair(w_b, w_a, c_b, ca_b)
    backed = adjoint_pair(t_a, t_b, c_a[:, :, 1:-1], ca_a[:, 1:-1])
    return moved, backed


def coupling(coefs, first_row):
    return jnp.where(first_row, coefs[3], coefs[4])


def localize(members, search, loc_cols, loc_vals, partials):
    count_members = members.shape[0]
    block = members.shape[-1]
    products = (members.astype(jnp.float32) * search[None]).astype(jnp.bfloat16)
    flat = products.reshape(-1, block)
    rows = flat.shape[0]
    bands = lax.axis_size("lon")
    here = lax.axis_index("lon")
    even = here % 2 == 0
    columns = loc_cols[0]
    tiles = loc_vals[0]
    partner = [(i, i ^ 1) for i in range(bands)]
    beside = lax.ppermute(flat, "lon", partner)
    ahead = from_offset(flat, "lon", 2)
    behind = from_offset(flat, "lon", -2)
    far = lax.ppermute(flat, "lon", [(s, (s + 3) % bands if s % 2 else (s - 3) % bands) for s in range(bands)])
    relayed = lax.ppermute(jnp.concatenate([ahead, behind], axis=0), "lon", partner)
    received = [
        (beside, jnp.where(even, 1, -1)),
        (ahead, 2),
        (behind, -2),
        (far, jnp.where(even, -3, 3)),
        (relayed[:rows], jnp.where(even, 3, 1)),
        (relayed[rows:], jnp.where(even, -1, -3)),
    ]

    def weight_for(offset):
        target = (here + offset + bands) % bands
        match = columns == target
        picked = tiles[jnp.argmax(match)]
        return jnp.where(jnp.any(match), picked, jnp.zeros_like(picked))

    partials, _ = lax.optimization_barrier((partials, [value for value, _ in received]))
    total = jnp.dot(flat, weight_for(0), preferred_element_type=jnp.float32)
    for value, offset in received:
        total = total + jnp.dot(value, weight_for(offset), preferred_element_type=jnp.float32)
    spread = total.reshape(products.shape)
    return jnp.sum(members.astype(jnp.float32) * spread, axis=0) / (count_members - 1), partials


def local(
    dual_state,
    dual_obs,
    increment,
    resid_dual,
    resid_obs,
    resid_incr,
    search_dual,
    search_obs,
    search_incr,
    ensemble,
    tangent_coefs,
    obs_weight,
    obs_var,
    loc_cols,
    loc_vals,
):
    resid_local = (
        jnp.sum(resid_dual * resid_dual)
        + jnp.sum(resid_obs * resid_obs)
        + jnp.sum(resid_incr * resid_incr)
    )
    search_local = (
        jnp.sum(search_dual * search_dual)
        + jnp.sum(search_obs * search_obs)
        + jnp.sum(search_incr * search_incr)
    )

    packed = jnp.concatenate(
        [search_incr[0, :, 0][None], search_dual[0, :, 0][None], tangent_coefs[0, :, :, 0]], axis=0
    )
    own = lon_extended(packed, 2)
    first_row = lax.axis_index("lat") == 0
    other = lat_partner(jnp.concatenate([own[:5], coupling(own[2:], first_row)[None]]))
    moved, backed = propagate_both(own, other, first_row)
    earlier = shifted(moved.astype(jnp.bfloat16), "win", 1).astype(jnp.float32)[None, :, None]
    following = shifted(backed.astype(jnp.bfloat16), "win", -1).astype(jnp.float32)[None, :, None]

    covar, partials = localize(
        ensemble[0, :, :, 0],
        search_dual[0, :, 0],
        loc_cols,
        loc_vals,
        butterfly_sum(jnp.stack([resid_local, search_local]), ("win",)),
    )
    covar = covar[None, :, None]
    partials, _ = lax.optimization_barrier((partials, other))
    sums = butterfly_sum(partials, ("lon", "lat"))
    alpha = sums[0] / (sums[1] + 1e-06)
    image_dual = covar + search_incr - earlier
    image_obs = obs_var * search_obs + obs_weight * search_incr
    image_incr = search_dual - following + obs_weight * search_obs
    return (
        dual_state + alpha * search_dual,
        dual_obs + alpha * search_obs,
        increment + alpha * search_incr,
        resid_dual - alpha * image_dual,
        resid_obs - alpha * image_obs,
        resid_incr - alpha * image_incr,
    )


def solution(mesh):
    field = P("win", None, "lat", "lon")
    stacked = P("win", None, None, "lat", "lon")
    placed = (
        field, field, field, field, field, field, field, field, field,
        stacked, stacked, field, field,
        P("lon", None),
        P("lon", None, None, None),
    )
    return jax.shard_map(
        local,
        mesh=mesh,
        in_specs=placed,
        out_specs=(field,) * 6,
        check_vma=False,
    )
```

```python
import jax
import jax.numpy as jnp
from jax import lax
from jax.sharding import PartitionSpec as P

REACH = 3


def from_offset(value, axis, distance):
    count = lax.axis_size(axis)
    return lax.ppermute(value, axis, [((i + distance) % count, i) for i in range(count)])


def shifted(value, axis, steps):
    count = lax.axis_size(axis)
    leading, last = (max(0, -steps), min(count, count - steps))
    return lax.ppermute(value, axis, [(source, source + steps) for source in range(leading, last)])


def butterfly_sum(value, axes):
    for axis in axes:
        count = lax.axis_size(axis)
        step = 1
        while step < count:
            value = value + lax.ppermute(value, axis, [(i, i ^ step) for i in range(count)])
            step *= 2
    return value


def lon_extended(packed, width):
    left = from_offset(packed[..., -width:], "lon", -1)
    right = from_offset(packed[..., :width], "lon", 1)
    return jnp.concatenate([left, packed, right], axis=-1)


def lat_partner(value):
    return lax.ppermute(value, "lat", [(0, 1), (1, 0)])


def forward_pair(f_a, f_b, c_a, cn_a):
    return (
        (0.5 + c_a[0, :, 1:-1]) * f_a[:, 1:-1]
        + c_a[1, :, 1:-1] * f_a[:, 2:]
        + c_a[2, :, 1:-1] * f_a[:, :-2]
        + cn_a[:, 1:-1] * f_b[:, 1:-1]
    )


def adjoint_pair(f_a, f_b, c_a, ca_a):
    return (
        (0.5 + c_a[0, :, 1:-1]) * f_a[:, 1:-1]
        + (c_a[1] * f_a)[:, :-2]
        + (c_a[2] * f_a)[:, 2:]
        + ca_a[:, 1:-1] * f_b[:, 1:-1]
    )


def propagate_both(own, other, first_row):
    u_a, w_a, c_a = own[0], own[1], own[2:]
    u_b, w_b, c_b, k_b = other[0], other[1], other[2:5], other[5]
    cn_a = coupling(own[2:], first_row)
    cn_b = k_b
    ca_a = k_b
    ca_b = cn_a
    s_a = forward_pair(u_a, u_b, c_a, cn_a)
    s_b = forward_pair(u_b, u_a, c_b, cn_b)
    moved = forward_pair(s_a, s_b, c_a[:, :, 1:-1], cn_a[:, 1:-1])
    t_a = adjoint_pair(w_a, w_b, c_a, ca_a)
    t_b = adjoint_pair(w_b, w_a, c_b, ca_b)
    backed = adjoint_pair(t_a, t_b, c_a[:, :, 1:-1], ca_a[:, 1:-1])
    return moved, backed


def coupling(coefs, first_row):
    return jnp.where(first_row, coefs[3], coefs[4])


def localize(members, search, loc_cols, loc_vals, partials):
    count_members = members.shape[0]
    block = members.shape[-1]
    products = (members.astype(jnp.float32) * search[None]).astype(jnp.bfloat16)
    flat = products.reshape(-1, block)
    rows = flat.shape[0]
    bands = lax.axis_size("lon")
    here = lax.axis_index("lon")
    even = here % 2 == 0
    columns = loc_cols[0]
    tiles = loc_vals[0]
    partner = [(i, i ^ 1) for i in range(bands)]
    beside = lax.ppermute(flat, "lon", partner)
    ahead = from_offset(flat, "lon", 2)
    behind = from_offset(flat, "lon", -2)
    far = lax.ppermute(flat, "lon", [(s, (s + 3) % bands if s % 2 else (s - 3) % bands) for s in range(bands)])
    relayed = lax.ppermute(jnp.concatenate([ahead, behind], axis=0), "lon", partner)
    received = [
        (beside, jnp.where(even, 1, -1)),
        (ahead, 2),
        (behind, -2),
        (far, jnp.where(even, -3, 3)),
        (relayed[:rows], jnp.where(even, 3, 1)),
        (relayed[rows:], jnp.where(even, -1, -3)),
    ]

    def weight_for(offset):
        target = (here + offset + bands) % bands
        match = columns == target
        picked = tiles[jnp.argmax(match)]
        return jnp.where(jnp.any(match), picked, jnp.zeros_like(picked))

    partials, _ = lax.optimization_barrier((partials, [value for value, _ in received]))
    total = jnp.dot(flat, weight_for(0), preferred_element_type=jnp.float32)
    for value, offset in received:
        total = total + jnp.dot(value, weight_for(offset), preferred_element_type=jnp.float32)
    spread = total.reshape(products.shape)
    return jnp.sum(members.astype(jnp.float32) * spread, axis=0) / (count_members - 1), partials


def local(
    dual_state,
    dual_obs,
    increment,
    resid_dual,
    resid_obs,
    resid_incr,
    search_dual,
    search_obs,
    search_incr,
    ensemble,
    tangent_coefs,
    obs_weight,
    obs_var,
    loc_cols,
    loc_vals,
):
    resid_local = (
        jnp.sum(resid_dual * resid_dual)
        + jnp.sum(resid_obs * resid_obs)
        + jnp.sum(resid_incr * resid_incr)
    )
    search_local = (
        jnp.sum(search_dual * search_dual)
        + jnp.sum(search_obs * search_obs)
        + jnp.sum(search_incr * search_incr)
    )

    packed = jnp.concatenate(
        [search_incr[0, :, 0][None], search_dual[0, :, 0][None], tangent_coefs[0, :, :, 0]], axis=0
    )
    own = lon_extended(packed, 2)
    first_row = lax.axis_index("lat") == 0
    other = lat_partner(
        jnp.concatenate([own[:5], coupling(own[2:], first_row)[None]]).astype(jnp.bfloat16)
    ).astype(jnp.float32)
    moved, backed = propagate_both(own, other, first_row)
    earlier = shifted(moved.astype(jnp.bfloat16), "win", 1).astype(jnp.float32)[None, :, None]
    following = shifted(backed.astype(jnp.bfloat16), "win", -1).astype(jnp.float32)[None, :, None]

    covar, partials = localize(
        ensemble[0, :, :, 0],
        search_dual[0, :, 0],
        loc_cols,
        loc_vals,
        butterfly_sum(jnp.stack([resid_local, search_local]), ("win",)),
    )
    covar = covar[None, :, None]
    partials, _ = lax.optimization_barrier((partials, other))
    sums = butterfly_sum(partials, ("lon", "lat"))
    alpha = sums[0] / (sums[1] + 1e-06)
    image_dual = covar + search_incr - earlier
    image_obs = obs_var * search_obs + obs_weight * search_incr
    image_incr = search_dual - following + obs_weight * search_obs
    return (
        dual_state + alpha * search_dual,
        dual_obs + alpha * search_obs,
        increment + alpha * search_incr,
        resid_dual - alpha * image_dual,
        resid_obs - alpha * image_obs,
        resid_incr - alpha * image_incr,
    )


def solution(mesh):
    field = P("win", None, "lat", "lon")
    stacked = P("win", None, None, "lat", "lon")
    placed = (
        field, field, field, field, field, field, field, field, field,
        stacked, stacked, field, field,
        P("lon", None),
        P("lon", None, None, None),
    )
    return jax.shard_map(
        local,
        mesh=mesh,
        in_specs=placed,
        out_specs=(field,) * 6,
        check_vma=False,
    )
```

```python
import jax
import jax.numpy as jnp
from jax import lax
from jax.sharding import PartitionSpec as P

REACH = 3


def from_offset(value, axis, distance):
    count = lax.axis_size(axis)
    return lax.ppermute(value, axis, [((i + distance) % count, i) for i in range(count)])


def shifted(value, axis, steps):
    count = lax.axis_size(axis)
    leading, last = (max(0, -steps), min(count, count - steps))
    return lax.ppermute(value, axis, [(source, source + steps) for source in range(leading, last)])


def butterfly_sum(value, axes):
    for axis in axes:
        count = lax.axis_size(axis)
        step = 1
        while step < count:
            value = value + lax.ppermute(value, axis, [(i, i ^ step) for i in range(count)])
            step *= 2
    return value


def lon_extended(packed, width):
    left = from_offset(packed[..., -width:], "lon", -1)
    right = from_offset(packed[..., :width], "lon", 1)
    return jnp.concatenate([left, packed, right], axis=-1)


def lat_partner(value):
    return lax.ppermute(value, "lat", [(0, 1), (1, 0)])


def forward_pair(f_a, f_b, c_a, cn_a):
    return (
        (0.5 + c_a[0, :, 1:-1]) * f_a[:, 1:-1]
        + c_a[1, :, 1:-1] * f_a[:, 2:]
        + c_a[2, :, 1:-1] * f_a[:, :-2]
        + cn_a[:, 1:-1] * f_b[:, 1:-1]
    )


def adjoint_pair(f_a, f_b, c_a, ca_a):
    return (
        (0.5 + c_a[0, :, 1:-1]) * f_a[:, 1:-1]
        + (c_a[1] * f_a)[:, :-2]
        + (c_a[2] * f_a)[:, 2:]
        + ca_a[:, 1:-1] * f_b[:, 1:-1]
    )


def propagate_both(own, other, first_row):
    u_a, w_a, c_a = own[0], own[1], own[2:]
    u_b, w_b, c_b, k_b = other[0], other[1], other[2:5], other[5]
    cn_a = coupling(own[2:], first_row)
    cn_b = k_b
    ca_a = k_b
    ca_b = cn_a
    s_a = forward_pair(u_a, u_b, c_a, cn_a)
    s_b = forward_pair(u_b, u_a, c_b, cn_b)
    moved = forward_pair(s_a, s_b, c_a[:, :, 1:-1], cn_a[:, 1:-1])
    t_a = adjoint_pair(w_a, w_b, c_a, ca_a)
    t_b = adjoint_pair(w_b, w_a, c_b, ca_b)
    backed = adjoint_pair(t_a, t_b, c_a[:, :, 1:-1], ca_a[:, 1:-1])
    return moved, backed


def coupling(coefs, first_row):
    return jnp.where(first_row, coefs[3], coefs[4])


def localize(members, search, loc_cols, loc_vals, partials):
    count_members = members.shape[0]
    block = members.shape[-1]
    products = (members.astype(jnp.float32) * search[None]).astype(jnp.bfloat16)
    flat = products.reshape(-1, block)
    rows = flat.shape[0]
    bands = lax.axis_size("lon")
    here = lax.axis_index("lon")
    even = here % 2 == 0
    columns = loc_cols[0]
    tiles = loc_vals[0]
    partner = [(i, i ^ 1) for i in range(bands)]
    beside = lax.ppermute(flat, "lon", partner)
    ahead = from_offset(flat, "lon", 2)
    behind = from_offset(flat, "lon", -2)
    far = lax.ppermute(flat, "lon", [(s, (s + 3) % bands if s % 2 else (s - 3) % bands) for s in range(bands)])
    relayed = lax.ppermute(jnp.concatenate([ahead, behind], axis=0), "lon", partner)
    received = [
        (beside, jnp.where(even, 1, -1)),
        (ahead, 2),
        (behind, -2),
        (far, jnp.where(even, -3, 3)),
        (relayed[:rows], jnp.where(even, 3, 1)),
        (relayed[rows:], jnp.where(even, -1, -3)),
    ]

    def weight_for(offset):
        target = (here + offset + bands) % bands
        match = columns == target
        picked = tiles[jnp.argmax(match)]
        return jnp.where(jnp.any(match), picked, jnp.zeros_like(picked))

    partials, _ = lax.optimization_barrier((partials, [value for value, _ in received]))
    total = jnp.dot(flat, weight_for(0), preferred_element_type=jnp.float32)
    for value, offset in received:
        total = total + jnp.dot(value, weight_for(offset), preferred_element_type=jnp.float32)
    spread = total.reshape(products.shape)
    return jnp.sum(members.astype(jnp.float32) * spread, axis=0) / (count_members - 1), partials


def local(
    dual_state,
    dual_obs,
    increment,
    resid_dual,
    resid_obs,
    resid_incr,
    search_dual,
    search_obs,
    search_incr,
    ensemble,
    tangent_coefs,
    obs_weight,
    obs_var,
    loc_cols,
    loc_vals,
):
    resid_local = (
        jnp.sum(resid_dual * resid_dual)
        + jnp.sum(resid_obs * resid_obs)
        + jnp.sum(resid_incr * resid_incr)
    )
    search_local = (
        jnp.sum(search_dual * search_dual)
        + jnp.sum(search_obs * search_obs)
        + jnp.sum(search_incr * search_incr)
    )

    packed = jnp.concatenate(
        [search_incr[0, :, 0][None], search_dual[0, :, 0][None], tangent_coefs[0, :, :, 0]], axis=0
    )
    own = lon_extended(packed, 2)
    first_row = lax.axis_index("lat") == 0
    six = jnp.concatenate([packed[:5], coupling(packed[2:], first_row)[None]]).astype(jnp.bfloat16)
    bands = lax.axis_size("lon")
    diagonal = [
        [(i * 2 + a, ((i + step) % bands) * 2 + 1 - a) for i in range(bands) for a in range(2)]
        for step in (1, -1)
    ]
    from_west = lax.ppermute(six[..., -2:], ("lon", "lat"), diagonal[0])
    from_east = lax.ppermute(six[..., :2], ("lon", "lat"), diagonal[1])
    other = jnp.concatenate([from_west, lat_partner(six), from_east], axis=-1).astype(jnp.float32)
    moved, backed = propagate_both(own, other, first_row)
    earlier = shifted(moved.astype(jnp.bfloat16), "win", 1).astype(jnp.float32)[None, :, None]
    following = shifted(backed.astype(jnp.bfloat16), "win", -1).astype(jnp.float32)[None, :, None]

    covar, partials = localize(
        ensemble[0, :, :, 0],
        search_dual[0, :, 0],
        loc_cols,
        loc_vals,
        butterfly_sum(jnp.stack([resid_local, search_local]), ("win",)),
    )
    covar = covar[None, :, None]
    partials, _ = lax.optimization_barrier((partials, other))
    sums = butterfly_sum(partials, ("lon", "lat"))
    alpha = sums[0] / (sums[1] + 1e-06)
    image_dual = covar + search_incr - earlier
    image_obs = obs_var * search_obs + obs_weight * search_incr
    image_incr = search_dual - following + obs_weight * search_obs
    return (
        dual_state + alpha * search_dual,
        dual_obs + alpha * search_obs,
        increment + alpha * search_incr,
        resid_dual - alpha * image_dual,
        resid_obs - alpha * image_obs,
        resid_incr - alpha * image_incr,
    )


def solution(mesh):
    field = P("win", None, "lat", "lon")
    stacked = P("win", None, None, "lat", "lon")
    placed = (
        field, field, field, field, field, field, field, field, field,
        stacked, stacked, field, field,
        P("lon", None),
        P("lon", None, None, None),
    )
    return jax.shard_map(
        local,
        mesh=mesh,
        in_specs=placed,
        out_specs=(field,) * 6,
        check_vma=False,
    )
```

```python
import jax
import jax.numpy as jnp
from jax import lax
from jax.sharding import PartitionSpec as P

REACH = 3


def from_offset(value, axis, distance):
    count = lax.axis_size(axis)
    return lax.ppermute(value, axis, [((i + distance) % count, i) for i in range(count)])


def shifted(value, axis, steps):
    count = lax.axis_size(axis)
    leading, last = (max(0, -steps), min(count, count - steps))
    return lax.ppermute(value, axis, [(source, source + steps) for source in range(leading, last)])


def butterfly_sum(value, axes):
    for axis in axes:
        count = lax.axis_size(axis)
        step = 1
        while step < count:
            value = value + lax.ppermute(value, axis, [(i, i ^ step) for i in range(count)])
            step *= 2
    return value


def lon_extended(packed, width):
    left = from_offset(packed[..., -width:], "lon", -1)
    right = from_offset(packed[..., :width], "lon", 1)
    return jnp.concatenate([left, packed, right], axis=-1)


def lat_partner(value):
    return lax.ppermute(value, "lat", [(0, 1), (1, 0)])


def forward_pair(f_a, f_b, c_a, cn_a):
    return (
        (0.5 + c_a[0, :, 1:-1]) * f_a[:, 1:-1]
        + c_a[1, :, 1:-1] * f_a[:, 2:]
        + c_a[2, :, 1:-1] * f_a[:, :-2]
        + cn_a[:, 1:-1] * f_b[:, 1:-1]
    )


def adjoint_pair(f_a, f_b, c_a, ca_a):
    return (
        (0.5 + c_a[0, :, 1:-1]) * f_a[:, 1:-1]
        + (c_a[1] * f_a)[:, :-2]
        + (c_a[2] * f_a)[:, 2:]
        + ca_a[:, 1:-1] * f_b[:, 1:-1]
    )


def propagate_both(own, other, first_row):
    u_a, w_a, c_a = own[0], own[1], own[2:]
    u_b, w_b, c_b, k_b = other[0], other[1], other[2:5], other[5]
    cn_a = coupling(own[2:], first_row)
    cn_b = k_b
    ca_a = k_b
    ca_b = cn_a
    s_a = forward_pair(u_a, u_b, c_a, cn_a)
    s_b = forward_pair(u_b, u_a, c_b, cn_b)
    moved = forward_pair(s_a, s_b, c_a[:, :, 1:-1], cn_a[:, 1:-1])
    t_a = adjoint_pair(w_a, w_b, c_a, ca_a)
    t_b = adjoint_pair(w_b, w_a, c_b, ca_b)
    backed = adjoint_pair(t_a, t_b, c_a[:, :, 1:-1], ca_a[:, 1:-1])
    return moved, backed


def coupling(coefs, first_row):
    return jnp.where(first_row, coefs[3], coefs[4])


def localize(members, search, loc_cols, loc_vals, partials, own):
    count_members = members.shape[0]
    block = members.shape[-1]
    products = (members.astype(jnp.float32) * search[None]).astype(jnp.bfloat16)
    flat = products.reshape(-1, block)
    rows = flat.shape[0]
    bands = lax.axis_size("lon")
    here = lax.axis_index("lon")
    even = here % 2 == 0
    columns = loc_cols[0]
    tiles = loc_vals[0]
    partner = [(i, i ^ 1) for i in range(bands)]
    beside = lax.ppermute(flat, "lon", partner)
    ahead = from_offset(flat, "lon", 2)
    behind = from_offset(flat, "lon", -2)
    far = lax.ppermute(flat, "lon", [(s, (s + 3) % bands if s % 2 else (s - 3) % bands) for s in range(bands)])
    relayed = lax.ppermute(jnp.concatenate([ahead, behind], axis=0), "lon", partner)
    received = [
        (beside, jnp.where(even, 1, -1)),
        (ahead, 2),
        (behind, -2),
        (far, jnp.where(even, -3, 3)),
        (relayed[:rows], jnp.where(even, 3, 1)),
        (relayed[rows:], jnp.where(even, -1, -3)),
    ]

    def weight_for(offset):
        target = (here + offset + bands) % bands
        match = columns == target
        picked = tiles[jnp.argmax(match)]
        return jnp.where(jnp.any(match), picked, jnp.zeros_like(picked))

    partials, own, _ = lax.optimization_barrier((partials, own, [value for value, _ in received]))
    total = jnp.dot(flat, weight_for(0), preferred_element_type=jnp.float32)
    for value, offset in received:
        total = total + jnp.dot(value, weight_for(offset), preferred_element_type=jnp.float32)
    spread = total.reshape(products.shape)
    return jnp.sum(members.astype(jnp.float32) * spread, axis=0) / (count_members - 1), partials, own


def local(
    dual_state,
    dual_obs,
    increment,
    resid_dual,
    resid_obs,
    resid_incr,
    search_dual,
    search_obs,
    search_incr,
    ensemble,
    tangent_coefs,
    obs_weight,
    obs_var,
    loc_cols,
    loc_vals,
):
    resid_local = (
        jnp.sum(resid_dual * resid_dual)
        + jnp.sum(resid_obs * resid_obs)
        + jnp.sum(resid_incr * resid_incr)
    )
    search_local = (
        jnp.sum(search_dual * search_dual)
        + jnp.sum(search_obs * search_obs)
        + jnp.sum(search_incr * search_incr)
    )

    packed = jnp.concatenate(
        [search_incr[0, :, 0][None], search_dual[0, :, 0][None], tangent_coefs[0, :, :, 0]], axis=0
    )
    own = lon_extended(packed, 2)
    first_row = lax.axis_index("lat") == 0
    covar, partials, own = localize(
        ensemble[0, :, :, 0],
        search_dual[0, :, 0],
        loc_cols,
        loc_vals,
        butterfly_sum(jnp.stack([resid_local, search_local]), ("win",)),
        own,
    )
    covar = covar[None, :, None]
    other = lat_partner(
        jnp.concatenate([own[:5], coupling(own[2:], first_row)[None]]).astype(jnp.bfloat16)
    ).astype(jnp.float32)
    moved, backed = propagate_both(own, other, first_row)
    earlier = shifted(moved.astype(jnp.bfloat16), "win", 1).astype(jnp.float32)[None, :, None]
    following = shifted(backed.astype(jnp.bfloat16), "win", -1).astype(jnp.float32)[None, :, None]
    sums = butterfly_sum(partials, ("lon", "lat"))
    alpha = sums[0] / (sums[1] + 1e-06)
    image_dual = covar + search_incr - earlier
    image_obs = obs_var * search_obs + obs_weight * search_incr
    image_incr = search_dual - following + obs_weight * search_obs
    return (
        dual_state + alpha * search_dual,
        dual_obs + alpha * search_obs,
        increment + alpha * search_incr,
        resid_dual - alpha * image_dual,
        resid_obs - alpha * image_obs,
        resid_incr - alpha * image_incr,
    )


def solution(mesh):
    field = P("win", None, "lat", "lon")
    stacked = P("win", None, None, "lat", "lon")
    placed = (
        field, field, field, field, field, field, field, field, field,
        stacked, stacked, field, field,
        P("lon", None),
        P("lon", None, None, None),
    )
    return jax.shard_map(
        local,
        mesh=mesh,
        in_specs=placed,
        out_specs=(field,) * 6,
        check_vma=False,
    )
```

```python
import jax
import jax.numpy as jnp
from jax import lax
from jax.sharding import PartitionSpec as P

REACH = 3


def from_offset(value, axis, distance):
    count = lax.axis_size(axis)
    return lax.ppermute(value, axis, [((i + distance) % count, i) for i in range(count)])


def shifted(value, axis, steps):
    count = lax.axis_size(axis)
    leading, last = (max(0, -steps), min(count, count - steps))
    return lax.ppermute(value, axis, [(source, source + steps) for source in range(leading, last)])


def butterfly_sum(value, axes):
    for axis in axes:
        count = lax.axis_size(axis)
        step = 1
        while step < count:
            value = value + lax.ppermute(value, axis, [(i, i ^ step) for i in range(count)])
            step *= 2
    return value


def lon_extended(packed, width):
    left = from_offset(packed[..., -width:], "lon", -1)
    right = from_offset(packed[..., :width], "lon", 1)
    return jnp.concatenate([left, packed, right], axis=-1)


def lat_partner(value):
    return lax.ppermute(value, "lat", [(0, 1), (1, 0)])


def forward_pair(f_a, f_b, c_a, cn_a):
    return (
        (0.5 + c_a[0, :, 1:-1]) * f_a[:, 1:-1]
        + c_a[1, :, 1:-1] * f_a[:, 2:]
        + c_a[2, :, 1:-1] * f_a[:, :-2]
        + cn_a[:, 1:-1] * f_b[:, 1:-1]
    )


def adjoint_pair(f_a, f_b, c_a, ca_a):
    return (
        (0.5 + c_a[0, :, 1:-1]) * f_a[:, 1:-1]
        + (c_a[1] * f_a)[:, :-2]
        + (c_a[2] * f_a)[:, 2:]
        + ca_a[:, 1:-1] * f_b[:, 1:-1]
    )


def propagate_both(own, other, first_row):
    u_a, w_a, c_a = own[0], own[1], own[2:]
    u_b, w_b, c_b, k_b = other[0], other[1], other[2:5], other[5]
    cn_a = coupling(own[2:], first_row)
    cn_b = k_b
    ca_a = k_b
    ca_b = cn_a
    s_a = forward_pair(u_a, u_b, c_a, cn_a)
    s_b = forward_pair(u_b, u_a, c_b, cn_b)
    moved = forward_pair(s_a, s_b, c_a[:, :, 1:-1], cn_a[:, 1:-1])
    t_a = adjoint_pair(w_a, w_b, c_a, ca_a)
    t_b = adjoint_pair(w_b, w_a, c_b, ca_b)
    backed = adjoint_pair(t_a, t_b, c_a[:, :, 1:-1], ca_a[:, 1:-1])
    return moved, backed


def coupling(coefs, first_row):
    return jnp.where(first_row, coefs[3], coefs[4])


def localize(members, search, loc_cols, loc_vals, partials):
    count_members = members.shape[0]
    block = members.shape[-1]
    products = (members.astype(jnp.float32) * search[None]).astype(jnp.bfloat16)
    flat = products.reshape(-1, block)
    rows = flat.shape[0]
    bands = lax.axis_size("lon")
    here = lax.axis_index("lon")
    even = here % 2 == 0
    columns = loc_cols[0]
    tiles = loc_vals[0]
    partner = [(i, i ^ 1) for i in range(bands)]
    ahead = from_offset(flat, "lon", 2)
    behind = from_offset(flat, "lon", -2)
    late, _, _ = lax.optimization_barrier((flat, ahead, behind))
    beside = lax.ppermute(late, "lon", partner)
    far = lax.ppermute(late, "lon", [(s, (s + 3) % bands if s % 2 else (s - 3) % bands) for s in range(bands)])
    relayed = lax.ppermute(jnp.concatenate([ahead, behind], axis=0), "lon", partner)
    received = [
        (beside, jnp.where(even, 1, -1)),
        (ahead, 2),
        (behind, -2),
        (far, jnp.where(even, -3, 3)),
        (relayed[:rows], jnp.where(even, 3, 1)),
        (relayed[rows:], jnp.where(even, -1, -3)),
    ]

    def weight_for(offset):
        target = (here + offset + bands) % bands
        match = columns == target
        picked = tiles[jnp.argmax(match)]
        return jnp.where(jnp.any(match), picked, jnp.zeros_like(picked))

    partials, _ = lax.optimization_barrier((partials, [value for value, _ in received]))
    total = jnp.dot(flat, weight_for(0), preferred_element_type=jnp.float32)
    for value, offset in received:
        total = total + jnp.dot(value, weight_for(offset), preferred_element_type=jnp.float32)
    spread = total.reshape(products.shape)
    return jnp.sum(members.astype(jnp.float32) * spread, axis=0) / (count_members - 1), partials


def local(
    dual_state,
    dual_obs,
    increment,
    resid_dual,
    resid_obs,
    resid_incr,
    search_dual,
    search_obs,
    search_incr,
    ensemble,
    tangent_coefs,
    obs_weight,
    obs_var,
    loc_cols,
    loc_vals,
):
    resid_local = (
        jnp.sum(resid_dual * resid_dual)
        + jnp.sum(resid_obs * resid_obs)
        + jnp.sum(resid_incr * resid_incr)
    )
    search_local = (
        jnp.sum(search_dual * search_dual)
        + jnp.sum(search_obs * search_obs)
        + jnp.sum(search_incr * search_incr)
    )

    packed = jnp.concatenate(
        [search_incr[0, :, 0][None], search_dual[0, :, 0][None], tangent_coefs[0, :, :, 0]], axis=0
    )
    own = lon_extended(packed, 2)
    first_row = lax.axis_index("lat") == 0
    other = lat_partner(
        jnp.concatenate([own[:5], coupling(own[2:], first_row)[None]]).astype(jnp.bfloat16)
    ).astype(jnp.float32)
    moved, backed = propagate_both(own, other, first_row)
    earlier = shifted(moved.astype(jnp.bfloat16), "win", 1).astype(jnp.float32)[None, :, None]
    following = shifted(backed.astype(jnp.bfloat16), "win", -1).astype(jnp.float32)[None, :, None]

    covar, partials = localize(
        ensemble[0, :, :, 0],
        search_dual[0, :, 0],
        loc_cols,
        loc_vals,
        butterfly_sum(jnp.stack([resid_local, search_local]), ("win",)),
    )
    covar = covar[None, :, None]
    partials, _ = lax.optimization_barrier((partials, other))
    sums = butterfly_sum(partials, ("lon", "lat"))
    alpha = sums[0] / (sums[1] + 1e-06)
    image_dual = covar + search_incr - earlier
    image_obs = obs_var * search_obs + obs_weight * search_incr
    image_incr = search_dual - following + obs_weight * search_obs
    return (
        dual_state + alpha * search_dual,
        dual_obs + alpha * search_obs,
        increment + alpha * search_incr,
        resid_dual - alpha * image_dual,
        resid_obs - alpha * image_obs,
        resid_incr - alpha * image_incr,
    )


def solution(mesh):
    field = P("win", None, "lat", "lon")
    stacked = P("win", None, None, "lat", "lon")
    placed = (
        field, field, field, field, field, field, field, field, field,
        stacked, stacked, field, field,
        P("lon", None),
        P("lon", None, None, None),
    )
    return jax.shard_map(
        local,
        mesh=mesh,
        in_specs=placed,
        out_specs=(field,) * 6,
        check_vma=False,
    )
```
